256 devices in a mesh: ctx: 16 (over z_lo, x, core), tp: 16 (over z_hi, y).
Axes of the slice: x: 4, y: 4, z: 8 (z_hi: 4, z_lo: 2; z = z_hi * 2 + z_lo), core: 2. Of those that a mesh axis runs over, the one named last changes fastest.
Arguments:
- tokens: bfloat16 [8192, 8192], P('ctx'), may hold values from -40 to 40
- doc_lengths: int32 [8], replicated, may hold values from 1 to 4096, 8192 in all
- w_query: bfloat16 [8192, 4096], P('ctx', 'tp'), may hold values from -0.0625 to 0.0625
- w_key: bfloat16 [8192, 512], P('ctx', 'tp'), may hold values from -0.0625 to 0.0625
- w_value: bfloat16 [8192, 512], P('ctx', 'tp'), may hold values from -0.0625 to 0.0625
- w_output: bfloat16 [4096, 8192], P('tp', 'ctx'), may hold values from -0.09375 to 0.09375
Outputs:
- layer_out: bfloat16 [8192, 8192], P(('ctx', 'tp'))
The draws below stay inside these ranges and needn't reach their ends.
Inputs may be any that keep to these rules, and one draw needn't show every extreme that they name: `doc_lengths`: the 8 documents lie in order in the sequence, their lengths sum to 8192 and the longest has exactly 4096 tokens.
All inputs are finite; a program needn't handle non-finite values.
Results may differ from the reference program's by a relative error of at most 0.015.
Values may be sent and summed in bfloat16 or wider, within the bound.
No kernel may reach another device: no remote copies, remote signals or barrier semaphores. Data moves between devices by JAX's collectives and lax.ppermute only.
A program may use at most 64 MiB of HBM per device.

```python
import math
import jax
import jax.numpy as jnp
import numpy as np
from jax import lax

D = 8192
HD = 128
HEADS = 32
KVH = 4
NDOCS = 8
SEQ = 8192
DOC_MOST = 4096
N_TP = 16


def draw_tokens(key, part):
    noise_key = jax.random.fold_in(key, 11)
    noise = jax.random.normal(noise_key, (SEQ, D), jnp.float32)
    return jnp.clip(noise, -6.0, 6.0).astype(jnp.bfloat16)


def level_of(rng, dims, pieces, low, high):
    def one(dim, parts):
        steps = jax.random.uniform(jax.random.fold_in(jax.random.fold_in(rng, 6), dim), (parts,), jnp.float32, low / len(pieces), high / len(pieces))
        return jnp.repeat(jnp.exp(steps), dims[dim] // parts).reshape((-1,) + (1,) * (len(dims) - dim - 1))

    level = one(*pieces[0])
    for cut in pieces[1:]:
        level = level * one(*cut)
    return level


def split_up(count, total, limit, slope):
    weights = [(1 << 20) // math.isqrt(rank ** slope) + 1 for rank in range(2, count + 1)]
    spare, counts = total - limit - (count - 1), [1] * (count - 1)
    while spare > 0:
        movable = [i for i in range(count - 1) if counts[i] < limit]
        pool, left = sum([weights[i] for i in movable]), spare
        for i in movable:
            addition = min(limit - counts[i], max(1, left * weights[i] // pool), spare)
            counts[i] = counts[i] + addition
            spare = spare - addition
    return np.array([limit] + counts)


def ragged_sizes(stream_key, count, total, limit, slope):
    if count == 2:
        one = jax.random.randint(stream_key, (), max(1, total - limit), min(limit, total - 1) + 1)
        return jnp.stack([one, total - one])
    tallies = jnp.asarray(split_up(count, total, limit, slope), jnp.int32)
    couples = (count - 1) // 2
    donor, receiver = tallies[1:1 + 2 * couples:2], tallies[2:2 + 2 * couples:2]
    slack = jnp.minimum(donor - 1, limit - receiver)
    moved = jax.random.randint(jax.random.fold_in(stream_key, 1), (couples,), 0, 1 << 20) % (slack + 1)
    tallies = tallies.at[1:1 + 2 * couples:2].set(donor - moved).at[2:2 + 2 * couples:2].set(receiver + moved)
    return tallies[jax.random.permutation(jax.random.fold_in(stream_key, 2), count)]


def bell_draw(stream_key, dims, deviation, limit, split=(), held_as=jnp.bfloat16):
    drawn = jax.random.normal(stream_key, dims, jnp.float32) * deviation
    if len(split) > 0:
        drawn = level_of(stream_key, dims, split, -0.22, 0.18) * drawn
    return jnp.clip(drawn, min=-limit, max=limit).astype(held_as)


def setup_inputs(seed: int = 0) -> dict:
    splits = jax.random.split(jax.random.key(seed), 7)
    tokens = draw_tokens(jax.random.fold_in(splits[6], 71), 0)
    doc_lengths = ragged_sizes(splits[1], NDOCS, SEQ, DOC_MOST, 2).astype(jnp.int32)
    w_query = bell_draw(splits[2], (D, HEADS * HD), D ** -0.5, 0.0625, ((0, 16), (1, 16)))
    w_key = bell_draw(splits[3], (D, KVH * HD), D ** -0.5, 0.0625, ((0, 16), (1, 16)))
    w_value = bell_draw(splits[4], (D, KVH * HD), D ** -0.5, 0.0625, ((0, 16), (1, 16)))
    w_output = bell_draw(splits[5], (HEADS * HD, D), (HEADS * HD) ** -0.5, 0.09375, ((0, 16), (1, 16)))
    return dict(tokens=tokens, doc_lengths=doc_lengths, w_query=w_query, w_key=w_key, w_value=w_value, w_output=w_output)


rope_base = 500000.0


def rotate(field, positions):
    half_dim = field.shape[-1] // 2
    inverse_freq = rope_base ** (-2.0 * jnp.arange(half_dim, dtype=jnp.float32) / field.shape[-1])
    angles = positions.astype(jnp.float32)[:, None] * inverse_freq[None, :]
    cosine = jnp.cos(angles)[:, None, :]
    sine_part = jnp.sin(angles)[:, None, :]
    first_half = field[..., :half_dim]
    second_half = field[..., half_dim:]
    return jnp.concatenate([first_half * cosine - second_half * sine_part, second_half * cosine + first_half * sine_part], axis=-1)


def reference(tokens, doc_lengths, w_query, w_key, w_value, w_output):
    positions = jnp.arange(SEQ, dtype=jnp.int32)
    doc_starts = jnp.cumsum(doc_lengths).astype(jnp.int32) - doc_lengths
    doc_id = jnp.sum((positions[:, None] >= doc_starts[None, :]).astype(jnp.int32), axis=1)
    query_raw = jnp.dot(tokens, w_query, preferred_element_type=jnp.float32).reshape(SEQ, HEADS, HD)
    query = rotate(query_raw, positions).astype(jnp.bfloat16)
    key_raw = jnp.dot(tokens, w_key, preferred_element_type=jnp.float32).astype(jnp.bfloat16).reshape(SEQ, HD, KVH)
    key_raw = jnp.transpose(key_raw, (0, 2, 1))
    key_rot = rotate(key_raw.astype(jnp.float32), positions).astype(jnp.bfloat16)
    value = jnp.dot(tokens, w_value, preferred_element_type=jnp.float32).astype(jnp.bfloat16).reshape(SEQ, HD, KVH)
    value = jnp.transpose(value, (0, 2, 1))
    allowed = (positions[None, :] <= positions[:, None]) & (doc_id[None, :] == doc_id[:, None])
    group_size = HEADS // KVH
    score_scale = HD ** -0.5

    def one_head(head):
        query_head = lax.dynamic_index_in_dim(query, head, 1, keepdims=False).astype(jnp.float32)
        kv_head = head // group_size
        key_head = lax.dynamic_index_in_dim(key_rot, kv_head, 1, keepdims=False).astype(jnp.float32)
        value_head = lax.dynamic_index_in_dim(value, kv_head, 1, keepdims=False).astype(jnp.float32)
        scores = jnp.dot(query_head, key_head.T, preferred_element_type=jnp.float32) * score_scale
        masked = jnp.where(allowed, scores, -jnp.inf)
        row_max = jnp.max(masked, axis=1, keepdims=True)
        expo = jnp.where(allowed, jnp.exp(masked - row_max), 0.0)
        row_total = jnp.sum(expo, axis=1, keepdims=True)
        weights = lax.optimization_barrier(expo.astype(jnp.bfloat16)).astype(jnp.float32)
        mixed = jnp.dot(weights, value_head, preferred_element_type=jnp.float32) / row_total
        return mixed.astype(jnp.bfloat16)

    per_head = lax.map(one_head, jnp.arange(HEADS, dtype=jnp.int32))
    attended = jnp.transpose(per_head, (1, 0, 2)).reshape(SEQ, HEADS * HD)
    group_cols = HEADS * HD // N_TP
    attended_groups = jnp.transpose(attended.reshape(SEQ, N_TP, group_cols), (1, 0, 2))
    output_groups = w_output.reshape(N_TP, group_cols, D)

    def add_group(running, pair):
        partial_sum = jnp.dot(pair[0], pair[1], preferred_element_type=jnp.float32)
        partial_sum = lax.optimization_barrier(partial_sum.astype(jnp.bfloat16)).astype(jnp.float32)
        return running + partial_sum, None

    summed, _ = lax.scan(add_group, jnp.zeros((SEQ, D), jnp.float32), (attended_groups, output_groups))
    return summed.astype(jnp.bfloat16)
```

```python
import jax
import jax.numpy as jnp
from jax import lax
from jax.sharding import PartitionSpec as P

HD = 128
HEADS = 32
KVH = 4
DOC_MOST = 4096

rope_base = 500000.0


def rotate(field, positions):
    half_dim = field.shape[-1] // 2
    inverse_freq = rope_base ** (-2.0 * jnp.arange(half_dim, dtype=jnp.float32) / field.shape[-1])
    angles = positions.astype(jnp.float32)[:, None] * inverse_freq[None, :]
    cosine = jnp.cos(angles)[:, None, :]
    sine_part = jnp.sin(angles)[:, None, :]
    first_half = field[..., :half_dim]
    second_half = field[..., half_dim:]
    return jnp.concatenate(
        [
            first_half * cosine - second_half * sine_part,
            second_half * cosine + first_half * sine_part,
        ],
        axis=-1,
    )


def doc_of(positions, doc_starts):
    return jnp.sum((positions[:, None] >= doc_starts[None, :]).astype(jnp.int32), axis=1)


def on_device(tokens, doc_lengths, w_query, w_key, w_value, w_output):
    tok_rows = tokens.shape[0]
    n_tp = lax.axis_size("tp")
    ctx_index = lax.axis_index("ctx")
    tp_index = lax.axis_index("tp")
    first_row = ctx_index * tok_rows
    positions = first_row + jnp.arange(tok_rows, dtype=jnp.int32)
    doc_starts = jnp.cumsum(doc_lengths) - doc_lengths
    doc_ids = doc_of(positions, doc_starts)

    q_cols = w_query.shape[1]
    k_cols = w_key.shape[1]
    w_all = jnp.concatenate([w_query, w_key, w_value], axis=1)
    w_full = lax.all_gather(w_all, "ctx", axis=0, tiled=True)
    proj = jnp.dot(tokens, w_full, preferred_element_type=jnp.float32)
    query_sum = proj[:, :q_cols]
    kv_local = proj[:, q_cols:].astype(jnp.bfloat16)

    heads_dev = q_cols // HD
    query = rotate(query_sum.reshape(tok_rows, heads_dev, HD), positions).astype(jnp.bfloat16)

    kv_parts = lax.all_gather(kv_local, "tp", axis=0, tiled=False)
    dd = k_cols // KVH
    kv_head = tp_index * heads_dev // (HEADS // KVH)
    kv_parts = kv_parts.reshape(n_tp, tok_rows, 2, dd, KVH)
    kv_own = lax.dynamic_index_in_dim(kv_parts, kv_head, 4, keepdims=False)
    kv_own = jnp.transpose(kv_own, (1, 2, 0, 3)).reshape(tok_rows, 2, n_tp * dd)
    key_raw = kv_own[:, 0, :]
    value_own = kv_own[:, 1, :]
    key_rot = rotate(key_raw.astype(jnp.float32)[:, None, :], positions)[:, 0, :].astype(jnp.bfloat16)

    kv_rows_local = jnp.concatenate([key_rot, value_own], axis=1)
    kv_rows = lax.all_gather(kv_rows_local, "ctx", axis=0, tiled=True)
    seq = kv_rows.shape[0]

    window_blocks = min(seq // tok_rows, -(-(DOC_MOST - 1) // tok_rows) + 1)
    window = window_blocks * tok_rows
    start_block = jnp.clip(ctx_index - (window_blocks - 1), 0, seq // tok_rows - window_blocks)
    key_start = start_block * tok_rows
    kv_win = lax.dynamic_slice_in_dim(kv_rows, key_start, window, 0)
    key_win = kv_win[:, :HD]
    value_win = kv_win[:, HD:]
    key_positions = key_start + jnp.arange(window, dtype=jnp.int32)
    key_docs = doc_of(key_positions, doc_starts)

    score_scale = HD ** (-0.5)
    n_split = 2
    part_rows = tok_rows // n_split
    q_parts = jnp.transpose(query, (1, 0, 2)).reshape(heads_dev * n_split, part_rows, HD)
    pos_parts = jnp.tile(positions.reshape(n_split, part_rows), (heads_dev, 1))
    doc_parts = jnp.tile(doc_ids.reshape(n_split, part_rows), (heads_dev, 1))

    def one_part(args):
        q_part, pos_part, doc_part = args
        allowed = (key_positions[None, :] <= pos_part[:, None]) & (key_docs[None, :] == doc_part[:, None])
        scores = jnp.dot(q_part, key_win.T, preferred_element_type=jnp.float32) * score_scale
        masked = jnp.where(allowed, scores, -jnp.inf)
        row_max = jnp.max(masked, axis=-1, keepdims=True)
        expo = jnp.where(allowed, jnp.exp(masked - row_max), 0.0)
        row_total = jnp.sum(expo, axis=-1, keepdims=True)
        mixed = jnp.dot(expo.astype(jnp.bfloat16), value_win, preferred_element_type=jnp.float32)
        return (mixed / row_total).astype(jnp.bfloat16)

    attended = lax.map(one_part, (q_parts, pos_parts, doc_parts))
    attended = attended.reshape(heads_dev, tok_rows, HD)
    attended = jnp.transpose(attended, (1, 0, 2)).reshape(tok_rows, heads_dev * HD)

    output_full = lax.all_gather(w_output, "ctx", axis=1, tiled=True)
    return lax.psum_scatter(
        jnp.dot(attended, output_full, preferred_element_type=jnp.float32).astype(jnp.bfloat16),
        "tp",
        scatter_dimension=0,
        tiled=True,
    )


def solution(mesh):
    placed = (P("ctx", None), P(), P("ctx", "tp"), P("ctx", "tp"), P("ctx", "tp"), P("tp", "ctx"))
    return jax.shard_map(
        on_device, mesh=mesh, in_specs=placed, out_specs=P(("ctx", "tp"), None), check_vma=False
    )
```

```python
import jax
import jax.numpy as jnp
from jax import lax
from jax.sharding import PartitionSpec as P

HD = 128
HEADS = 32
KVH = 4
DOC_MOST = 4096

rope_base = 500000.0


def rotate(field, positions):
    half_dim = field.shape[-1] // 2
    inverse_freq = rope_base ** (-2.0 * jnp.arange(half_dim, dtype=jnp.float32) / field.shape[-1])
    angles = positions.astype(jnp.float32)[:, None] * inverse_freq[None, :]
    cosine = jnp.cos(angles)[:, None, :]
    sine_part = jnp.sin(angles)[:, None, :]
    first_half = field[..., :half_dim]
    second_half = field[..., half_dim:]
    return jnp.concatenate(
        [
            first_half * cosine - second_half * sine_part,
            second_half * cosine + first_half * sine_part,
        ],
        axis=-1,
    )


def doc_of(positions, doc_starts):
    return jnp.sum((positions[:, None] >= doc_starts[None, :]).astype(jnp.int32), axis=1)


def on_device(tokens, doc_lengths, w_query, w_key, w_value, w_output):
    tok_rows = tokens.shape[0]
    n_tp = lax.axis_size("tp")
    ctx_index = lax.axis_index("ctx")
    tp_index = lax.axis_index("tp")
    first_row = ctx_index * tok_rows
    positions = first_row + jnp.arange(tok_rows, dtype=jnp.int32)
    doc_starts = jnp.cumsum(doc_lengths) - doc_lengths
    doc_ids = doc_of(positions, doc_starts)

    q_cols = w_query.shape[1]
    k_cols = w_key.shape[1]
    w_all = jnp.concatenate([w_query, w_key, w_value], axis=1)
    w_full = lax.all_gather(w_all, "ctx", axis=0, tiled=True)
    proj = jnp.dot(tokens, w_full, preferred_element_type=jnp.float32)
    query_sum = proj[:, :q_cols]
    kv_local = proj[:, q_cols:].astype(jnp.bfloat16)

    heads_dev = q_cols // HD
    query = rotate(query_sum.reshape(tok_rows, heads_dev, HD), positions).astype(jnp.bfloat16)

    dd = k_cols // KVH
    group = HEADS // KVH
    kv_local = kv_local.reshape(tok_rows, 2, dd, KVH)
    dest_heads = jnp.arange(n_tp, dtype=jnp.int32) * heads_dev // group
    pieces = jnp.take(kv_local, dest_heads, axis=3)
    pieces = jnp.transpose(pieces, (3, 0, 1, 2))
    got = lax.all_to_all(pieces, "tp", 0, 0, tiled=False)
    kv_own = jnp.transpose(got, (1, 2, 0, 3)).reshape(tok_rows, 2, n_tp * dd)
    key_raw = kv_own[:, 0, :]
    value_own = kv_own[:, 1, :]
    key_rot = rotate(key_raw.astype(jnp.float32)[:, None, :], positions)[:, 0, :].astype(jnp.bfloat16)
    kv_rows_local = jnp.concatenate([key_rot, value_own], axis=1)

    n_ctx = lax.axis_size("ctx")
    back = min(n_ctx - 1, -(-(DOC_MOST - 1) // tok_rows))
    slots = []
    for shift in range(back, 0, -1):
        slots.append(
            lax.ppermute(kv_rows_local, "ctx", [(i, i + shift) for i in range(n_ctx - shift)])
        )
    slots.append(kv_rows_local)
    kv_win = jnp.concatenate(slots, axis=0)
    window = kv_win.shape[0]
    key_start = (ctx_index - back) * tok_rows
    key_win = kv_win[:, :HD]
    value_win = kv_win[:, HD:]
    key_positions = key_start + jnp.arange(window, dtype=jnp.int32)
    key_docs = jnp.where(key_positions >= 0, doc_of(key_positions, doc_starts), -1)

    score_scale = HD ** (-0.5)
    n_split = 2
    part_rows = tok_rows // n_split
    q_parts = jnp.transpose(query, (1, 0, 2)).reshape(heads_dev * n_split, part_rows, HD)
    pos_parts = jnp.tile(positions.reshape(n_split, part_rows), (heads_dev, 1))
    doc_parts = jnp.tile(doc_ids.reshape(n_split, part_rows), (heads_dev, 1))

    def one_part(args):
        q_part, pos_part, doc_part = args
        allowed = (key_positions[None, :] <= pos_part[:, None]) & (key_docs[None, :] == doc_part[:, None])
        scores = jnp.dot(q_part, key_win.T, preferred_element_type=jnp.float32) * score_scale
        masked = jnp.where(allowed, scores, -jnp.inf)
        row_max = jnp.max(masked, axis=-1, keepdims=True)
        expo = jnp.where(allowed, jnp.exp(masked - row_max), 0.0)
        row_total = jnp.sum(expo, axis=-1, keepdims=True)
        mixed = jnp.dot(expo.astype(jnp.bfloat16), value_win, preferred_element_type=jnp.float32)
        return (mixed / row_total).astype(jnp.bfloat16)

    attended = lax.map(one_part, (q_parts, pos_parts, doc_parts))
    attended = attended.reshape(heads_dev, tok_rows, HD)
    attended = jnp.transpose(attended, (1, 0, 2)).reshape(tok_rows, heads_dev * HD)

    output_full = lax.all_gather(w_output, "ctx", axis=1, tiled=True)
    return lax.psum_scatter(
        jnp.dot(attended, output_full, preferred_element_type=jnp.float32).astype(jnp.bfloat16),
        "tp",
        scatter_dimension=0,
        tiled=True,
    )


def solution(mesh):
    placed = (P("ctx", None), P(), P("ctx", "tp"), P("ctx", "tp"), P("ctx", "tp"), P("tp", "ctx"))
    return jax.shard_map(
        on_device, mesh=mesh, in_specs=placed, out_specs=P(("ctx", "tp"), None), check_vma=False
    )
```

```python
import jax
import jax.numpy as jnp
from jax import lax
from jax.sharding import PartitionSpec as P

HD = 128
HEADS = 32
KVH = 4
DOC_MOST = 4096

rope_base = 500000.0


def rotate(field, positions):
    half_dim = field.shape[-1] // 2
    inverse_freq = rope_base ** (-2.0 * jnp.arange(half_dim, dtype=jnp.float32) / field.shape[-1])
    angles = positions.astype(jnp.float32)[:, None] * inverse_freq[None, :]
    cosine = jnp.cos(angles)[:, None, :]
    sine_part = jnp.sin(angles)[:, None, :]
    first_half = field[..., :half_dim]
    second_half = field[..., half_dim:]
    return jnp.concatenate(
        [
            first_half * cosine - second_half * sine_part,
            second_half * cosine + first_half * sine_part,
        ],
        axis=-1,
    )


def doc_of(positions, doc_starts):
    return jnp.sum((positions[:, None] >= doc_starts[None, :]).astype(jnp.int32), axis=1)


def on_device(tokens, doc_lengths, w_query, w_key, w_value, w_output):
    tok_rows = tokens.shape[0]
    n_tp = lax.axis_size("tp")
    ctx_index = lax.axis_index("ctx")
    tp_index = lax.axis_index("tp")
    first_row = ctx_index * tok_rows
    positions = first_row + jnp.arange(tok_rows, dtype=jnp.int32)
    doc_starts = jnp.cumsum(doc_lengths) - doc_lengths
    doc_ids = doc_of(positions, doc_starts)

    q_cols = w_query.shape[1]
    k_cols = w_key.shape[1]
    w_all = jnp.concatenate([w_query, w_key, w_value], axis=1)
    w_full = lax.all_gather(w_all, "ctx", axis=0, tiled=True)
    proj = jnp.dot(tokens, w_full, preferred_element_type=jnp.float32)
    query_sum = proj[:, :q_cols]
    kv_local = proj[:, q_cols:].astype(jnp.bfloat16)

    heads_dev = q_cols // HD
    query = rotate(query_sum.reshape(tok_rows, heads_dev, HD), positions).astype(jnp.bfloat16)

    dd = k_cols // KVH
    group = HEADS // KVH
    kv_local = kv_local.reshape(tok_rows, 2, dd, KVH)
    dest_heads = jnp.arange(n_tp, dtype=jnp.int32) * heads_dev // group
    pieces = jnp.take(kv_local, dest_heads, axis=3)
    pieces = jnp.transpose(pieces, (3, 0, 1, 2))
    got = lax.all_to_all(pieces, "tp", 0, 0, tiled=False)
    kv_own = jnp.transpose(got, (1, 2, 0, 3)).reshape(tok_rows, 2, n_tp * dd)
    key_raw = kv_own[:, 0, :]
    value_own = kv_own[:, 1, :]
    key_rot = rotate(key_raw.astype(jnp.float32)[:, None, :], positions)[:, 0, :].astype(jnp.bfloat16)
    kv_rows_local = jnp.concatenate([key_rot, value_own], axis=1)

    n_ctx = lax.axis_size("ctx")
    back = min(n_ctx - 1, -(-(DOC_MOST - 1) // tok_rows))
    slots = []
    for shift in range(back, 0, -1):
        slots.append(
            lax.ppermute(kv_rows_local, "ctx", [(i, i + shift) for i in range(n_ctx - shift)])
        )
    slots.append(kv_rows_local)
    kv_win = jnp.concatenate(slots, axis=0)
    window = kv_win.shape[0]
    key_start = (ctx_index - back) * tok_rows
    key_win = kv_win[:, :HD]
    value_win = kv_win[:, HD:]
    key_positions = key_start + jnp.arange(window, dtype=jnp.int32)
    key_docs = jnp.where(key_positions >= 0, doc_of(key_positions, doc_starts), -1)

    score_scale = HD ** (-0.5)
    n_split = 2
    part_rows = tok_rows // n_split
    q_parts = jnp.transpose(query, (1, 0, 2)).reshape(heads_dev * n_split, part_rows, HD)
    pos_parts = jnp.tile(positions.reshape(n_split, part_rows), (heads_dev, 1))
    doc_parts = jnp.tile(doc_ids.reshape(n_split, part_rows), (heads_dev, 1))

    def one_part(args):
        q_part, pos_part, doc_part = args
        allowed = (key_positions[None, :] <= pos_part[:, None]) & (key_docs[None, :] == doc_part[:, None])
        scores = jnp.dot(q_part, key_win.T, preferred_element_type=jnp.float32) * score_scale
        masked = jnp.where(allowed, scores, -jnp.inf)
        row_max = jnp.max(masked, axis=-1, keepdims=True)
        expo = jnp.where(allowed, jnp.exp(masked - row_max), 0.0)
        row_total = jnp.sum(expo, axis=-1, keepdims=True)
        mixed = jnp.dot(expo.astype(jnp.bfloat16), value_win, preferred_element_type=jnp.float32)
        return (mixed / row_total).astype(jnp.bfloat16)

    attended = lax.map(one_part, (q_parts, pos_parts, doc_parts))
    attended = attended.reshape(heads_dev, tok_rows, HD)
    attended = jnp.transpose(attended, (1, 0, 2)).reshape(tok_rows, heads_dev * HD)

    n_ctx_all = lax.axis_size("ctx")
    w_moved = lax.ppermute(
        w_output,
        ("ctx", "tp"),
        [(c * n_tp + t, t * n_tp + c) for c in range(n_ctx_all) for t in range(n_tp)],
    )
    w_chunk = lax.all_gather(w_moved, "ctx", axis=0, tiled=True)
    attended_all = lax.all_gather(attended, "tp", axis=1, tiled=True)
    out_chunk = jnp.dot(attended_all, w_chunk, preferred_element_type=jnp.float32).astype(jnp.bfloat16)
    chunk = out_chunk.shape[1]
    out_rows = tok_rows // n_tp
    sent = out_chunk.reshape(n_tp, out_rows, chunk)
    got_rows = lax.all_to_all(sent, "tp", 0, 0, tiled=False)
    return jnp.transpose(got_rows, (1, 0, 2)).reshape(out_rows, n_tp * chunk)


def solution(mesh):
    placed = (P("ctx", None), P(), P("ctx", "tp"), P("ctx", "tp"), P("ctx", "tp"), P("tp", "ctx"))
    return jax.shard_map(
        on_device, mesh=mesh, in_specs=placed, out_specs=P(("ctx", "tp"), None), check_vma=False
    )
```

```python
import jax
import jax.numpy as jnp
from jax import lax
from jax.sharding import PartitionSpec as P

HD = 128
HEADS = 32
KVH = 4
DOC_MOST = 4096

rope_base = 500000.0


def rotate(field, positions):
    half_dim = field.shape[-1] // 2
    inverse_freq = rope_base ** (-2.0 * jnp.arange(half_dim, dtype=jnp.float32) / field.shape[-1])
    angles = positions.astype(jnp.float32)[:, None] * inverse_freq[None, :]
    cosine = jnp.cos(angles)[:, None, :]
    sine_part = jnp.sin(angles)[:, None, :]
    first_half = field[..., :half_dim]
    second_half = field[..., half_dim:]
    return jnp.concatenate(
        [
            first_half * cosine - second_half * sine_part,
            second_half * cosine + first_half * sine_part,
        ],
        axis=-1,
    )


def doc_of(positions, doc_starts):
    return jnp.sum((positions[:, None] >= doc_starts[None, :]).astype(jnp.int32), axis=1)


def on_device(tokens, doc_lengths, w_query, w_key, w_value, w_output):
    tok_rows = tokens.shape[0]
    n_tp = lax.axis_size("tp")
    ctx_index = lax.axis_index("ctx")
    tp_index = lax.axis_index("tp")
    first_row = ctx_index * tok_rows
    positions = first_row + jnp.arange(tok_rows, dtype=jnp.int32)
    doc_starts = jnp.cumsum(doc_lengths) - doc_lengths
    doc_ids = doc_of(positions, doc_starts)

    q_cols = w_query.shape[1]
    k_cols = w_key.shape[1]
    w_kv = jnp.concatenate([w_key, w_value], axis=1)
    w_kv_full = lax.all_gather(w_kv, "ctx", axis=0, tiled=True)
    kv_local = jnp.dot(tokens, w_kv_full, preferred_element_type=jnp.float32).astype(jnp.bfloat16)
    w_q_full = lax.all_gather(w_query, "ctx", axis=0, tiled=True)
    query_sum = jnp.dot(tokens, w_q_full, preferred_element_type=jnp.float32)

    heads_dev = q_cols // HD
    query = rotate(query_sum.reshape(tok_rows, heads_dev, HD), positions).astype(jnp.bfloat16)

    dd = k_cols // KVH
    group = HEADS // KVH
    kv_local = kv_local.reshape(tok_rows, 2, dd, KVH)
    dest_heads = jnp.arange(n_tp, dtype=jnp.int32) * heads_dev // group
    pieces = jnp.take(kv_local, dest_heads, axis=3)
    pieces = jnp.transpose(pieces, (3, 0, 1, 2))
    got = lax.all_to_all(pieces, "tp", 0, 0, tiled=False)
    kv_own = jnp.transpose(got, (1, 2, 0, 3)).reshape(tok_rows, 2, n_tp * dd)
    key_raw = kv_own[:, 0, :]
    value_own = kv_own[:, 1, :]
    key_rot = rotate(key_raw.astype(jnp.float32)[:, None, :], positions)[:, 0, :].astype(jnp.bfloat16)
    kv_rows_local = jnp.concatenate([key_rot, value_own], axis=1)

    n_ctx = lax.axis_size("ctx")
    back = min(n_ctx - 1, -(-(DOC_MOST - 1) // tok_rows))
    slots = []
    for shift in range(back, 0, -1):
        slots.append(
            lax.ppermute(kv_rows_local, "ctx", [(i, i + shift) for i in range(n_ctx - shift)])
        )
    slots.append(kv_rows_local)
    kv_win = jnp.concatenate(slots, axis=0)
    window = kv_win.shape[0]
    key_start = (ctx_index - back) * tok_rows
    key_win = kv_win[:, :HD]
    value_win = kv_win[:, HD:]
    key_positions = key_start + jnp.arange(window, dtype=jnp.int32)
    key_docs = jnp.where(key_positions >= 0, doc_of(key_positions, doc_starts), -1)

    score_scale = HD ** (-0.5)
    n_split = 2
    part_rows = tok_rows // n_split
    q_parts = jnp.transpose(query, (1, 0, 2)).reshape(heads_dev * n_split, part_rows, HD)
    pos_parts = jnp.tile(positions.reshape(n_split, part_rows), (heads_dev, 1))
    doc_parts = jnp.tile(doc_ids.reshape(n_split, part_rows), (heads_dev, 1))

    def one_part(args):
        q_part, pos_part, doc_part = args
        allowed = (key_positions[None, :] <= pos_part[:, None]) & (key_docs[None, :] == doc_part[:, None])
        scores = jnp.dot(q_part, key_win.T, preferred_element_type=jnp.float32) * score_scale
        masked = jnp.where(allowed, scores, -jnp.inf)
        row_max = jnp.max(masked, axis=-1, keepdims=True)
        expo = jnp.where(allowed, jnp.exp(masked - row_max), 0.0)
        row_total = jnp.sum(expo, axis=-1, keepdims=True)
        mixed = jnp.dot(expo.astype(jnp.bfloat16), value_win, preferred_element_type=jnp.float32)
        return (mixed / row_total).astype(jnp.bfloat16)

    attended = lax.map(one_part, (q_parts, pos_parts, doc_parts))
    attended = attended.reshape(heads_dev, tok_rows, HD)
    attended = jnp.transpose(attended, (1, 0, 2)).reshape(tok_rows, heads_dev * HD)

    n_ctx_all = lax.axis_size("ctx")
    w_moved = lax.ppermute(
        w_output,
        ("ctx", "tp"),
        [(c * n_tp + t, t * n_tp + c) for c in range(n_ctx_all) for t in range(n_tp)],
    )
    w_chunk = lax.all_gather(w_moved, "ctx", axis=0, tiled=True)
    attended_all = lax.all_gather(attended, "tp", axis=1, tiled=True)
    out_chunk = jnp.dot(attended_all, w_chunk, preferred_element_type=jnp.float32).astype(jnp.bfloat16)
    chunk = out_chunk.shape[1]
    out_rows = tok_rows // n_tp
    sent = out_chunk.reshape(n_tp, out_rows, chunk)
    got_rows = lax.all_to_all(sent, "tp", 0, 0, tiled=False)
    return jnp.transpose(got_rows, (1, 0, 2)).reshape(out_rows, n_tp * chunk)


def solution(mesh):
    placed = (P("ctx", None), P(), P("ctx", "tp"), P("ctx", "tp"), P("ctx", "tp"), P("tp", "ctx"))
    return jax.shard_map(
        on_device, mesh=mesh, in_specs=placed, out_specs=P(("ctx", "tp"), None), check_vma=False
    )
```

```python
import jax
import jax.numpy as jnp
from jax import lax
from jax.sharding import PartitionSpec as P

HD = 128
HEADS = 32
KVH = 4
DOC_MOST = 4096

rope_base = 500000.0


def rotate(field, positions):
    half_dim = field.shape[-1] // 2
    inverse_freq = rope_base ** (-2.0 * jnp.arange(half_dim, dtype=jnp.float32) / field.shape[-1])
    angles = positions.astype(jnp.float32)[:, None] * inverse_freq[None, :]
    cosine = jnp.cos(angles)[:, None, :]
    sine_part = jnp.sin(angles)[:, None, :]
    first_half = field[..., :half_dim]
    second_half = field[..., half_dim:]
    return jnp.concatenate(
        [
            first_half * cosine - second_half * sine_part,
            second_half * cosine + first_half * sine_part,
        ],
        axis=-1,
    )


def doc_of(positions, doc_starts):
    return jnp.sum((positions[:, None] >= doc_starts[None, :]).astype(jnp.int32), axis=1)


def on_device(tokens, doc_lengths, w_query, w_key, w_value, w_output):
    tok_rows = tokens.shape[0]
    n_tp = lax.axis_size("tp")
    ctx_index = lax.axis_index("ctx")
    tp_index = lax.axis_index("tp")
    first_row = ctx_index * tok_rows
    positions = first_row + jnp.arange(tok_rows, dtype=jnp.int32)
    doc_starts = jnp.cumsum(doc_lengths) - doc_lengths
    doc_ids = doc_of(positions, doc_starts)

    q_cols = w_query.shape[1]
    k_cols = w_key.shape[1]
    w_kv = jnp.concatenate([w_key, w_value], axis=1)
    w_kv_full = lax.all_gather(w_kv, "ctx", axis=0, tiled=True)
    kv_local = jnp.dot(tokens, w_kv_full, preferred_element_type=jnp.float32).astype(jnp.bfloat16)
    w_q_full = lax.all_gather(w_query, "ctx", axis=0, tiled=True)
    query_sum = jnp.dot(tokens, w_q_full, preferred_element_type=jnp.float32)

    heads_dev = q_cols // HD
    query = rotate(query_sum.reshape(tok_rows, heads_dev, HD), positions).astype(jnp.bfloat16)

    dd = k_cols // KVH
    group = HEADS // KVH
    kv_local = kv_local.reshape(tok_rows, 2, dd, KVH)
    dest_heads = jnp.arange(n_tp, dtype=jnp.int32) * heads_dev // group
    pieces = jnp.take(kv_local, dest_heads, axis=3)
    pieces = jnp.transpose(pieces, (3, 0, 1, 2))
    got = lax.all_to_all(pieces, "tp", 0, 0, tiled=False)
    kv_own = jnp.transpose(got, (1, 2, 0, 3)).reshape(tok_rows, 2, n_tp * dd)
    key_raw = kv_own[:, 0, :]
    value_own = kv_own[:, 1, :]
    key_rot = rotate(key_raw.astype(jnp.float32)[:, None, :], positions)[:, 0, :].astype(jnp.bfloat16)
    kv_rows_local = jnp.concatenate([key_rot, value_own], axis=1)

    n_ctx = lax.axis_size("ctx")
    back = min(n_ctx - 1, -(-(DOC_MOST - 1) // tok_rows))
    slots = []
    for shift in range(back, 0, -1):
        slots.append(
            lax.ppermute(kv_rows_local, "ctx", [(i, i + shift) for i in range(n_ctx - shift)])
        )
    slots.append(kv_rows_local)
    kv_win = jnp.concatenate(slots, axis=0)
    window = kv_win.shape[0]
    key_start = (ctx_index - back) * tok_rows
    key_win = kv_win[:, :HD]
    value_win = kv_win[:, HD:]
    key_positions = key_start + jnp.arange(window, dtype=jnp.int32)
    key_docs = jnp.where(key_positions >= 0, doc_of(key_positions, doc_starts), -1)

    score_scale = HD ** (-0.5)
    n_split = 2
    part_rows = tok_rows // n_split
    q_parts = jnp.transpose(query, (1, 0, 2)).reshape(heads_dev * n_split, part_rows, HD)
    pos_parts = jnp.tile(positions.reshape(n_split, part_rows), (heads_dev, 1))
    doc_parts = jnp.tile(doc_ids.reshape(n_split, part_rows), (heads_dev, 1))

    def one_part(args):
        q_part, pos_part, doc_part = args
        allowed = (key_positions[None, :] <= pos_part[:, None]) & (key_docs[None, :] == doc_part[:, None])
        scores = jnp.dot(q_part, key_win.T, preferred_element_type=jnp.float32) * score_scale
        masked = jnp.where(allowed, scores, -jnp.inf)
        row_max = jnp.max(masked, axis=-1, keepdims=True)
        expo = jnp.where(allowed, jnp.exp(masked - row_max), 0.0)
        row_total = jnp.sum(expo, axis=-1, keepdims=True)
        mixed = jnp.dot(expo.astype(jnp.bfloat16), value_win, preferred_element_type=jnp.float32)
        return (mixed / row_total).astype(jnp.bfloat16)

    attended = lax.map(one_part, (q_parts, pos_parts, doc_parts))
    attended = attended.reshape(heads_dev, tok_rows, HD)
    attended = jnp.transpose(attended, (1, 0, 2)).reshape(tok_rows, heads_dev * HD)

    n_ctx_all = lax.axis_size("ctx")
    w_moved = lax.ppermute(
        w_output,
        ("ctx", "tp"),
        [(c * n_tp + t, t * n_tp + c) for c in range(n_ctx_all) for t in range(n_tp)],
    )
    w_chunk = lax.all_gather(w_moved, "ctx", axis=0, tiled=True)
    copies = jnp.broadcast_to(attended[None], (n_tp,) + attended.shape)
    from_peers = lax.all_to_all(copies, "tp", 0, 0, tiled=False)
    attended_all = jnp.transpose(from_peers, (1, 0, 2)).reshape(tok_rows, n_tp * attended.shape[1])
    out_chunk = jnp.dot(attended_all, w_chunk, preferred_element_type=jnp.float32).astype(jnp.bfloat16)
    chunk = out_chunk.shape[1]
    out_rows = tok_rows // n_tp
    sent = out_chunk.reshape(n_tp, out_rows, chunk)
    got_rows = lax.all_to_all(sent, "tp", 0, 0, tiled=False)
    return jnp.transpose(got_rows, (1, 0, 2)).reshape(out_rows, n_tp * chunk)


def solution(mesh):
    placed = (P("ctx", None), P(), P("ctx", "tp"), P("ctx", "tp"), P("ctx", "tp"), P("tp", "ctx"))
    return jax.shard_map(
        on_device, mesh=mesh, in_specs=placed, out_specs=P(("ctx", "tp"), None), check_vma=False
    )
```

```python
import jax
import jax.numpy as jnp
from jax import lax
from jax.sharding import PartitionSpec as P

HD = 128
HEADS = 32
KVH = 4
DOC_MOST = 4096

rope_base = 500000.0


def rotate(field, positions):
    half_dim = field.shape[-1] // 2
    inverse_freq = rope_base ** (-2.0 * jnp.arange(half_dim, dtype=jnp.float32) / field.shape[-1])
    angles = positions.astype(jnp.float32)[:, None] * inverse_freq[None, :]
    cosine = jnp.cos(angles)[:, None, :]
    sine_part = jnp.sin(angles)[:, None, :]
    first_half = field[..., :half_dim]
    second_half = field[..., half_dim:]
    return jnp.concatenate(
        [
            first_half * cosine - second_half * sine_part,
            second_half * cosine + first_half * sine_part,
        ],
        axis=-1,
    )


def doc_of(positions, doc_starts):
    return jnp.sum((positions[:, None] >= doc_starts[None, :]).astype(jnp.int32), axis=1)


def on_device(tokens, doc_lengths, w_query, w_key, w_value, w_output):
    tok_rows = tokens.shape[0]
    n_tp = lax.axis_size("tp")
    ctx_index = lax.axis_index("ctx")
    tp_index = lax.axis_index("tp")
    first_row = ctx_index * tok_rows
    positions = first_row + jnp.arange(tok_rows, dtype=jnp.int32)
    doc_starts = jnp.cumsum(doc_lengths) - doc_lengths
    doc_ids = doc_of(positions, doc_starts)

    q_cols = w_query.shape[1]
    k_cols = w_key.shape[1]
    w_kv = jnp.concatenate([w_key, w_value], axis=1)
    w_kv_full = lax.all_gather(w_kv, "ctx", axis=0, tiled=True)
    kv_local = jnp.dot(tokens, w_kv_full, preferred_element_type=jnp.float32).astype(jnp.bfloat16)
    n_ctx_all = lax.axis_size("ctx")
    w_moved = lax.ppermute(
        w_output,
        ("ctx", "tp"),
        [(c * n_tp + t, t * n_tp + c) for c in range(n_ctx_all) for t in range(n_tp)],
    )
    o_rows, o_cols = w_moved.shape
    w_q_o = jnp.concatenate([w_query, w_moved.reshape(tok_rows, o_rows * o_cols // tok_rows)], axis=1)
    w_q_o_full = lax.all_gather(w_q_o, "ctx", axis=0, tiled=False)
    w_q_full = w_q_o_full[:, :, :q_cols].reshape(n_ctx_all * tok_rows, q_cols)
    w_chunk = w_q_o_full[:, :, q_cols:].reshape(n_ctx_all * o_rows, o_cols)
    query_sum = jnp.dot(tokens, w_q_full, preferred_element_type=jnp.float32)

    heads_dev = q_cols // HD
    query = rotate(query_sum.reshape(tok_rows, heads_dev, HD), positions).astype(jnp.bfloat16)

    dd = k_cols // KVH
    group = HEADS // KVH
    kv_local = kv_local.reshape(tok_rows, 2, dd, KVH)
    dest_heads = jnp.arange(n_tp, dtype=jnp.int32) * heads_dev // group
    pieces = jnp.take(kv_local, dest_heads, axis=3)
    pieces = jnp.transpose(pieces, (3, 0, 1, 2))
    got = lax.all_to_all(pieces, "tp", 0, 0, tiled=False)
    kv_own = jnp.transpose(got, (1, 2, 0, 3)).reshape(tok_rows, 2, n_tp * dd)
    key_raw = kv_own[:, 0, :]
    value_own = kv_own[:, 1, :]
    key_rot = rotate(key_raw.astype(jnp.float32)[:, None, :], positions)[:, 0, :].astype(jnp.bfloat16)
    kv_rows_local = jnp.concatenate([key_rot, value_own], axis=1)

    n_ctx = lax.axis_size("ctx")
    back = min(n_ctx - 1, -(-(DOC_MOST - 1) // tok_rows))
    slots = []
    for shift in range(back, 0, -1):
        slots.append(
            lax.ppermute(kv_rows_local, "ctx", [(i, i + shift) for i in range(n_ctx - shift)])
        )
    slots.append(kv_rows_local)
    kv_win = jnp.concatenate(slots, axis=0)
    window = kv_win.shape[0]
    key_start = (ctx_index - back) * tok_rows
    key_win = kv_win[:, :HD]
    value_win = kv_win[:, HD:]
    key_positions = key_start + jnp.arange(window, dtype=jnp.int32)
    key_docs = jnp.where(key_positions >= 0, doc_of(key_positions, doc_starts), -1)

    score_scale = HD ** (-0.5)
    n_split = 2
    part_rows = tok_rows // n_split
    q_parts = jnp.transpose(query, (1, 0, 2)).reshape(heads_dev * n_split, part_rows, HD)
    pos_parts = jnp.tile(positions.reshape(n_split, part_rows), (heads_dev, 1))
    doc_parts = jnp.tile(doc_ids.reshape(n_split, part_rows), (heads_dev, 1))

    def one_part(args):
        q_part, pos_part, doc_part = args
        allowed = (key_positions[None, :] <= pos_part[:, None]) & (key_docs[None, :] == doc_part[:, None])
        scores = jnp.dot(q_part, key_win.T, preferred_element_type=jnp.float32) * score_scale
        masked = jnp.where(allowed, scores, -jnp.inf)
        row_max = jnp.max(masked, axis=-1, keepdims=True)
        expo = jnp.where(allowed, jnp.exp(masked - row_max), 0.0)
        row_total = jnp.sum(expo, axis=-1, keepdims=True)
        mixed = jnp.dot(expo.astype(jnp.bfloat16), value_win, preferred_element_type=jnp.float32)
        return (mixed / row_total).astype(jnp.bfloat16)

    attended = lax.map(one_part, (q_parts, pos_parts, doc_parts))
    attended = attended.reshape(heads_dev, tok_rows, HD)
    attended = jnp.transpose(attended, (1, 0, 2)).reshape(tok_rows, heads_dev * HD)

    attended_all = lax.all_gather(attended, "tp", axis=1, tiled=True)
    out_chunk = jnp.dot(attended_all, w_chunk, preferred_element_type=jnp.float32).astype(jnp.bfloat16)
    chunk = out_chunk.shape[1]
    out_rows = tok_rows // n_tp
    sent = out_chunk.reshape(n_tp, out_rows, chunk)
    got_rows = lax.all_to_all(sent, "tp", 0, 0, tiled=False)
    return jnp.transpose(got_rows, (1, 0, 2)).reshape(out_rows, n_tp * chunk)


def solution(mesh):
    placed = (P("ctx", None), P(), P("ctx", "tp"), P("ctx", "tp"), P("ctx", "tp"), P("tp", "ctx"))
    return jax.shard_map(
        on_device, mesh=mesh, in_specs=placed, out_specs=P(("ctx", "tp"), None), check_vma=False
    )
```

```python
import jax
import jax.numpy as jnp
from jax import lax
from jax.sharding import PartitionSpec as P

HD = 128
HEADS = 32
KVH = 4
DOC_MOST = 4096

rope_base = 500000.0


def rotate(field, positions):
    half_dim = field.shape[-1] // 2
    inverse_freq = rope_base ** (-2.0 * jnp.arange(half_dim, dtype=jnp.float32) / field.shape[-1])
    angles = positions.astype(jnp.float32)[:, None] * inverse_freq[None, :]
    cosine = jnp.cos(angles)[:, None, :]
    sine_part = jnp.sin(angles)[:, None, :]
    first_half = field[..., :half_dim]
    second_half = field[..., half_dim:]
    return jnp.concatenate(
        [
            first_half * cosine - second_half * sine_part,
            second_half * cosine + first_half * sine_part,
        ],
        axis=-1,
    )


def doc_of(positions, doc_starts):
    return jnp.sum((positions[:, None] >= doc_starts[None, :]).astype(jnp.int32), axis=1)


def on_device(tokens, doc_lengths, w_query, w_key, w_value, w_output):
    tok_rows = tokens.shape[0]
    n_tp = lax.axis_size("tp")
    ctx_index = lax.axis_index("ctx")
    tp_index = lax.axis_index("tp")
    first_row = ctx_index * tok_rows
    positions = first_row + jnp.arange(tok_rows, dtype=jnp.int32)
    doc_starts = jnp.cumsum(doc_lengths) - doc_lengths
    doc_ids = doc_of(positions, doc_starts)

    q_cols = w_query.shape[1]
    k_cols = w_key.shape[1]
    w_kv = jnp.concatenate([w_key, w_value], axis=1)
    n_ctx_all = lax.axis_size("ctx")
    ring = [w_kv]
    for shift in range(1, n_ctx_all):
        ring.append(lax.ppermute(w_kv, "ctx", [(i, (i + shift) % n_ctx_all) for i in range(n_ctx_all)]))
    ring = jnp.stack(ring)
    sources = (ctx_index - jnp.arange(n_ctx_all, dtype=jnp.int32)) % n_ctx_all
    w_kv_full = jnp.take(ring, sources, axis=0).reshape(n_ctx_all * tok_rows, w_kv.shape[1])
    kv_local = jnp.dot(tokens, w_kv_full, preferred_element_type=jnp.float32).astype(jnp.bfloat16)
    w_q_full = lax.all_gather(w_query, "ctx", axis=0, tiled=True)
    query_sum = jnp.dot(tokens, w_q_full, preferred_element_type=jnp.float32)

    heads_dev = q_cols // HD
    query = rotate(query_sum.reshape(tok_rows, heads_dev, HD), positions).astype(jnp.bfloat16)

    dd = k_cols // KVH
    group = HEADS // KVH
    kv_local = kv_local.reshape(tok_rows, 2, dd, KVH)
    dest_heads = jnp.arange(n_tp, dtype=jnp.int32) * heads_dev // group
    pieces = jnp.take(kv_local, dest_heads, axis=3)
    pieces = jnp.transpose(pieces, (3, 0, 1, 2))
    got = lax.all_to_all(pieces, "tp", 0, 0, tiled=False)
    kv_own = jnp.transpose(got, (1, 2, 0, 3)).reshape(tok_rows, 2, n_tp * dd)
    key_raw = kv_own[:, 0, :]
    value_own = kv_own[:, 1, :]
    key_rot = rotate(key_raw.astype(jnp.float32)[:, None, :], positions)[:, 0, :].astype(jnp.bfloat16)
    kv_rows_local = jnp.concatenate([key_rot, value_own], axis=1)

    n_ctx = lax.axis_size("ctx")
    back = min(n_ctx - 1, -(-(DOC_MOST - 1) // tok_rows))
    slots = []
    for shift in range(back, 0, -1):
        slots.append(
            lax.ppermute(kv_rows_local, "ctx", [(i, i + shift) for i in range(n_ctx - shift)])
        )
    slots.append(kv_rows_local)
    kv_win = jnp.concatenate(slots, axis=0)
    window = kv_win.shape[0]
    key_start = (ctx_index - back) * tok_rows
    key_win = kv_win[:, :HD]
    value_win = kv_win[:, HD:]
    key_positions = key_start + jnp.arange(window, dtype=jnp.int32)
    key_docs = jnp.where(key_positions >= 0, doc_of(key_positions, doc_starts), -1)

    score_scale = HD ** (-0.5)
    n_split = 2
    part_rows = tok_rows // n_split
    q_parts = jnp.transpose(query, (1, 0, 2)).reshape(heads_dev * n_split, part_rows, HD)
    pos_parts = jnp.tile(positions.reshape(n_split, part_rows), (heads_dev, 1))
    doc_parts = jnp.tile(doc_ids.reshape(n_split, part_rows), (heads_dev, 1))

    def one_part(args):
        q_part, pos_part, doc_part = args
        allowed = (key_positions[None, :] <= pos_part[:, None]) & (key_docs[None, :] == doc_part[:, None])
        scores = jnp.dot(q_part, key_win.T, preferred_element_type=jnp.float32) * score_scale
        masked = jnp.where(allowed, scores, -jnp.inf)
        row_max = jnp.max(masked, axis=-1, keepdims=True)
        expo = jnp.where(allowed, jnp.exp(masked - row_max), 0.0)
        row_total = jnp.sum(expo, axis=-1, keepdims=True)
        mixed = jnp.dot(expo.astype(jnp.bfloat16), value_win, preferred_element_type=jnp.float32)
        return (mixed / row_total).astype(jnp.bfloat16)

    attended = lax.map(one_part, (q_parts, pos_parts, doc_parts))
    attended = attended.reshape(heads_dev, tok_rows, HD)
    attended = jnp.transpose(attended, (1, 0, 2)).reshape(tok_rows, heads_dev * HD)

    w_moved = lax.ppermute(
        w_output,
        ("ctx", "tp"),
        [(c * n_tp + t, t * n_tp + c) for c in range(n_ctx_all) for t in range(n_tp)],
    )
    w_chunk = lax.all_gather(w_moved, "ctx", axis=0, tiled=True)
    attended_all = lax.all_gather(attended, "tp", axis=1, tiled=True)
    out_chunk = jnp.dot(attended_all, w_chunk, preferred_element_type=jnp.float32).astype(jnp.bfloat16)
    chunk = out_chunk.shape[1]
    out_rows = tok_rows // n_tp
    sent = out_chunk.reshape(n_tp, out_rows, chunk)
    got_rows = lax.all_to_all(sent, "tp", 0, 0, tiled=False)
    return jnp.transpose(got_rows, (1, 0, 2)).reshape(out_rows, n_tp * chunk)


def solution(mesh):
    placed = (P("ctx", None), P(), P("ctx", "tp"), P("ctx", "tp"), P("ctx", "tp"), P("tp", "ctx"))
    return jax.shard_map(
        on_device, mesh=mesh, in_specs=placed, out_specs=P(("ctx", "tp"), None), check_vma=False
    )
```

```python
import jax
import jax.numpy as jnp
from jax import lax
from jax.sharding import PartitionSpec as P

HD = 128
HEADS = 32
KVH = 4
DOC_MOST = 4096

rope_base = 500000.0


def rotate(field, positions):
    half_dim = field.shape[-1] // 2
    inverse_freq = rope_base ** (-2.0 * jnp.arange(half_dim, dtype=jnp.float32) / field.shape[-1])
    angles = positions.astype(jnp.float32)[:, None] * inverse_freq[None, :]
    cosine = jnp.cos(angles)[:, None, :]
    sine_part = jnp.sin(angles)[:, None, :]
    first_half = field[..., :half_dim]
    second_half = field[..., half_dim:]
    return jnp.concatenate(
        [
            first_half * cosine - second_half * sine_part,
            second_half * cosine + first_half * sine_part,
        ],
        axis=-1,
    )


def doc_of(positions, doc_starts):
    return jnp.sum((positions[:, None] >= doc_starts[None, :]).astype(jnp.int32), axis=1)


def on_device(tokens, doc_lengths, w_query, w_key, w_value, w_output):
    tok_rows = tokens.shape[0]
    n_tp = lax.axis_size("tp")
    ctx_index = lax.axis_index("ctx")
    tp_index = lax.axis_index("tp")
    first_row = ctx_index * tok_rows
    positions = first_row + jnp.arange(tok_rows, dtype=jnp.int32)
    doc_starts = jnp.cumsum(doc_lengths) - doc_lengths
    doc_ids = doc_of(positions, doc_starts)

    q_cols = w_query.shape[1]
    k_cols = w_key.shape[1]
    w_kv = jnp.concatenate([w_key, w_value], axis=1)
    n_ctx_all = lax.axis_size("ctx")
    ring = [w_kv]
    for shift in range(1, n_ctx_all):
        ring.append(lax.ppermute(w_kv, "ctx", [(i, (i + shift) % n_ctx_all) for i in range(n_ctx_all)]))
    ring = jnp.stack(ring)
    sources = (ctx_index - jnp.arange(n_ctx_all, dtype=jnp.int32)) % n_ctx_all
    w_kv_full = jnp.take(ring, sources, axis=0).reshape(n_ctx_all * tok_rows, w_kv.shape[1])
    kv_local = jnp.dot(tokens, w_kv_full, preferred_element_type=jnp.float32).astype(jnp.bfloat16)
    w_q_full = lax.all_gather(w_query, "ctx", axis=0, tiled=True)
    query_sum = jnp.dot(tokens, w_q_full, preferred_element_type=jnp.float32)

    heads_dev = q_cols // HD
    query = rotate(query_sum.reshape(tok_rows, heads_dev, HD), positions).astype(jnp.bfloat16)

    dd = k_cols // KVH
    group = HEADS // KVH
    kv_local = kv_local.reshape(tok_rows, 2, dd, KVH)
    dest_heads = jnp.arange(n_tp, dtype=jnp.int32) * heads_dev // group
    pieces = jnp.take(kv_local, dest_heads, axis=3)
    pieces = jnp.transpose(pieces, (3, 0, 1, 2))
    got = lax.all_to_all(pieces, "tp", 0, 0, tiled=False)
    kv_own = jnp.transpose(got, (1, 2, 0, 3)).reshape(tok_rows, 2, n_tp * dd)
    key_raw = kv_own[:, 0, :]
    value_own = kv_own[:, 1, :]
    key_rot = rotate(key_raw.astype(jnp.float32)[:, None, :], positions)[:, 0, :].astype(jnp.bfloat16)
    kv_rows_local = jnp.concatenate([key_rot, value_own], axis=1)
    kv_rows_local, query = lax.optimization_barrier((kv_rows_local, query))

    n_ctx = lax.axis_size("ctx")
    back = min(n_ctx - 1, -(-(DOC_MOST - 1) // tok_rows))
    slots = []
    for shift in range(back, 0, -1):
        slots.append(
            lax.ppermute(kv_rows_local, "ctx", [(i, i + shift) for i in range(n_ctx - shift)])
        )
    slots.append(kv_rows_local)
    kv_win = jnp.concatenate(slots, axis=0)
    window = kv_win.shape[0]
    key_start = (ctx_index - back) * tok_rows
    key_win = kv_win[:, :HD]
    value_win = kv_win[:, HD:]
    key_positions = key_start + jnp.arange(window, dtype=jnp.int32)
    key_docs = jnp.where(key_positions >= 0, doc_of(key_positions, doc_starts), -1)

    score_scale = HD ** (-0.5)
    n_split = 2
    part_rows = tok_rows // n_split
    q_parts = jnp.transpose(query, (1, 0, 2)).reshape(heads_dev * n_split, part_rows, HD)
    pos_parts = jnp.tile(positions.reshape(n_split, part_rows), (heads_dev, 1))
    doc_parts = jnp.tile(doc_ids.reshape(n_split, part_rows), (heads_dev, 1))

    def one_part(args):
        q_part, pos_part, doc_part = args
        allowed = (key_positions[None, :] <= pos_part[:, None]) & (key_docs[None, :] == doc_part[:, None])
        scores = jnp.dot(q_part, key_win.T, preferred_element_type=jnp.float32) * score_scale
        masked = jnp.where(allowed, scores, -jnp.inf)
        row_max = jnp.max(masked, axis=-1, keepdims=True)
        expo = jnp.where(allowed, jnp.exp(masked - row_max), 0.0)
        row_total = jnp.sum(expo, axis=-1, keepdims=True)
        mixed = jnp.dot(expo.astype(jnp.bfloat16), value_win, preferred_element_type=jnp.float32)
        return (mixed / row_total).astype(jnp.bfloat16)

    attended = lax.map(one_part, (q_parts, pos_parts, doc_parts))
    attended = attended.reshape(heads_dev, tok_rows, HD)
    attended = jnp.transpose(attended, (1, 0, 2)).reshape(tok_rows, heads_dev * HD)

    w_moved = lax.ppermute(
        w_output,
        ("ctx", "tp"),
        [(c * n_tp + t, t * n_tp + c) for c in range(n_ctx_all) for t in range(n_tp)],
    )
    w_chunk = lax.all_gather(w_moved, "ctx", axis=0, tiled=True)
    attended_all = lax.all_gather(attended, "tp", axis=1, tiled=True)
    out_chunk = jnp.dot(attended_all, w_chunk, preferred_element_type=jnp.float32).astype(jnp.bfloat16)
    chunk = out_chunk.shape[1]
    out_rows = tok_rows // n_tp
    sent = out_chunk.reshape(n_tp, out_rows, chunk)
    got_rows = lax.all_to_all(sent, "tp", 0, 0, tiled=False)
    return jnp.transpose(got_rows, (1, 0, 2)).reshape(out_rows, n_tp * chunk)


def solution(mesh):
    placed = (P("ctx", None), P(), P("ctx", "tp"), P("ctx", "tp"), P("ctx", "tp"), P("tp", "ctx"))
    return jax.shard_map(
        on_device, mesh=mesh, in_specs=placed, out_specs=P(("ctx", "tp"), None), check_vma=False
    )
```

```python
import jax
import jax.numpy as jnp
from jax import lax
from jax.sharding import PartitionSpec as P

HD = 128
HEADS = 32
KVH = 4
DOC_MOST = 4096

rope_base = 500000.0


def rotate(field, positions):
    half_dim = field.shape[-1] // 2
    inverse_freq = rope_base ** (-2.0 * jnp.arange(half_dim, dtype=jnp.float32) / field.shape[-1])
    angles = positions.astype(jnp.float32)[:, None] * inverse_freq[None, :]
    cosine = jnp.cos(angles)[:, None, :]
    sine_part = jnp.sin(angles)[:, None, :]
    first_half = field[..., :half_dim]
    second_half = field[..., half_dim:]
    return jnp.concatenate(
        [
            first_half * cosine - second_half * sine_part,
            second_half * cosine + first_half * sine_part,
        ],
        axis=-1,
    )


def doc_of(positions, doc_starts):
    return jnp.sum((positions[:, None] >= doc_starts[None, :]).astype(jnp.int32), axis=1)


def on_device(tokens, doc_lengths, w_query, w_key, w_value, w_output):
    tok_rows = tokens.shape[0]
    n_tp = lax.axis_size("tp")
    ctx_index = lax.axis_index("ctx")
    tp_index = lax.axis_index("tp")
    first_row = ctx_index * tok_rows
    positions = first_row + jnp.arange(tok_rows, dtype=jnp.int32)
    doc_starts = jnp.cumsum(doc_lengths) - doc_lengths
    doc_ids = doc_of(positions, doc_starts)

    q_cols = w_query.shape[1]
    k_cols = w_key.shape[1]
    w_kv = jnp.concatenate([w_key, w_value], axis=1)
    n_ctx_all = lax.axis_size("ctx")
    ring = [w_kv]
    for shift in range(1, n_ctx_all):
        ring.append(lax.ppermute(w_kv, "ctx", [(i, (i + shift) % n_ctx_all) for i in range(n_ctx_all)]))
    ring = jnp.stack(ring)
    sources = (ctx_index - jnp.arange(n_ctx_all, dtype=jnp.int32)) % n_ctx_all
    w_kv_full = jnp.take(ring, sources, axis=0).reshape(n_ctx_all * tok_rows, w_kv.shape[1])
    kv_local = jnp.dot(tokens, w_kv_full, preferred_element_type=jnp.float32).astype(jnp.bfloat16)
    w_q_full = lax.all_gather(w_query, "ctx", axis=0, tiled=True)
    query_sum = jnp.dot(tokens, w_q_full, preferred_element_type=jnp.float32)

    heads_dev = q_cols // HD
    query = rotate(query_sum.reshape(tok_rows, heads_dev, HD), positions).astype(jnp.bfloat16)

    dd = k_cols // KVH
    group = HEADS // KVH
    kv_local = kv_local.reshape(tok_rows, 2, dd, KVH)
    dest_heads = jnp.arange(n_tp, dtype=jnp.int32) * heads_dev // group
    pieces = jnp.take(kv_local, dest_heads, axis=3)
    pieces = jnp.transpose(pieces, (3, 0, 1, 2))
    got = lax.all_to_all(pieces, "tp", 0, 0, tiled=False)
    kv_own = jnp.transpose(got, (1, 2, 0, 3)).reshape(tok_rows, 2, n_tp * dd)
    key_raw = kv_own[:, 0, :]
    value_own = kv_own[:, 1, :]
    key_rot = rotate(key_raw.astype(jnp.float32)[:, None, :], positions)[:, 0, :].astype(jnp.bfloat16)
    kv_rows_local = jnp.concatenate([key_rot, value_own], axis=1)

    n_ctx = lax.axis_size("ctx")
    back = min(n_ctx - 1, -(-(DOC_MOST - 1) // tok_rows))
    slots = []
    for shift in range(back, 0, -1):
        slots.append(
            lax.ppermute(kv_rows_local, "ctx", [(i, i + shift) for i in range(n_ctx - shift)])
        )
    slots.append(kv_rows_local)
    kv_win = jnp.concatenate(slots, axis=0)
    window = kv_win.shape[0]
    key_start = (ctx_index - back) * tok_rows
    key_win = kv_win[:, :HD]
    value_win = kv_win[:, HD:]
    key_positions = key_start + jnp.arange(window, dtype=jnp.int32)
    key_docs = jnp.where(key_positions >= 0, doc_of(key_positions, doc_starts), -1)

    score_scale = HD ** (-0.5)
    n_split = 2
    part_rows = tok_rows // n_split
    q_parts = jnp.transpose(query, (1, 0, 2)).reshape(heads_dev * n_split, part_rows, HD)
    pos_parts = jnp.tile(positions.reshape(n_split, part_rows), (heads_dev, 1))
    doc_parts = jnp.tile(doc_ids.reshape(n_split, part_rows), (heads_dev, 1))

    def one_part(args):
        q_part, pos_part, doc_part = args
        allowed = (key_positions[None, :] <= pos_part[:, None]) & (key_docs[None, :] == doc_part[:, None])
        scores = jnp.dot(q_part, key_win.T, preferred_element_type=jnp.float32) * score_scale
        masked = jnp.where(allowed, scores, -jnp.inf)
        row_max = jnp.max(masked, axis=-1, keepdims=True)
        expo = jnp.where(allowed, jnp.exp(masked - row_max), 0.0)
        row_total = jnp.sum(expo, axis=-1, keepdims=True)
        mixed = jnp.dot(expo.astype(jnp.bfloat16), value_win, preferred_element_type=jnp.float32)
        return (mixed / row_total).astype(jnp.bfloat16)

    w_moved = lax.ppermute(
        w_output,
        ("ctx", "tp"),
        [(c * n_tp + t, t * n_tp + c) for c in range(n_ctx_all) for t in range(n_tp)],
    )
    w_chunk = lax.all_gather(w_moved, "ctx", axis=0, tiled=True)
    per_head = []
    for head in range(heads_dev):
        sl = slice(head * n_split, (head + 1) * n_split)
        one = lax.map(one_part, (q_parts[sl], pos_parts[sl], doc_parts[sl]))
        per_head.append(one.reshape(tok_rows, HD))
    first = heads_dev // 2
    early = jnp.stack(per_head[:first], axis=1)
    late = jnp.stack(per_head[first:], axis=1)
    early_all = lax.all_gather(early, "tp", axis=0, tiled=False)
    late_copies = jnp.broadcast_to(late[None], (n_tp,) + late.shape)
    late_all = lax.all_to_all(late_copies, "tp", 0, 0, tiled=False)
    both = jnp.concatenate([early_all, late_all], axis=2)
    attended_all = jnp.transpose(both, (1, 0, 2, 3)).reshape(tok_rows, n_tp * heads_dev * HD)
    out_chunk = jnp.dot(attended_all, w_chunk, preferred_element_type=jnp.float32).astype(jnp.bfloat16)
    chunk = out_chunk.shape[1]
    out_rows = tok_rows // n_tp
    sent = out_chunk.reshape(n_tp, out_rows, chunk)
    got_rows = lax.all_to_all(sent, "tp", 0, 0, tiled=False)
    return jnp.transpose(got_rows, (1, 0, 2)).reshape(out_rows, n_tp * chunk)


def solution(mesh):
    placed = (P("ctx", None), P(), P("ctx", "tp"), P("ctx", "tp"), P("ctx", "tp"), P("tp", "ctx"))
    return jax.shard_map(
        on_device, mesh=mesh, in_specs=placed, out_specs=P(("ctx", "tp"), None), check_vma=False
    )
```

```python
import jax
import jax.numpy as jnp
from jax import lax
from jax.sharding import PartitionSpec as P

HD = 128
HEADS = 32
KVH = 4
DOC_MOST = 4096

rope_base = 500000.0


def rotate(field, positions):
    half_dim = field.shape[-1] // 2
    inverse_freq = rope_base ** (-2.0 * jnp.arange(half_dim, dtype=jnp.float32) / field.shape[-1])
    angles = positions.astype(jnp.float32)[:, None] * inverse_freq[None, :]
    cosine = jnp.cos(angles)[:, None, :]
    sine_part = jnp.sin(angles)[:, None, :]
    first_half = field[..., :half_dim]
    second_half = field[..., half_dim:]
    return jnp.concatenate(
        [
            first_half * cosine - second_half * sine_part,
            second_half * cosine + first_half * sine_part,
        ],
        axis=-1,
    )


def doc_of(positions, doc_starts):
    return jnp.sum((positions[:, None] >= doc_starts[None, :]).astype(jnp.int32), axis=1)


def on_device(tokens, doc_lengths, w_query, w_key, w_value, w_output):
    tok_rows = tokens.shape[0]
    n_tp = lax.axis_size("tp")
    ctx_index = lax.axis_index("ctx")
    tp_index = lax.axis_index("tp")
    first_row = ctx_index * tok_rows
    positions = first_row + jnp.arange(tok_rows, dtype=jnp.int32)
    doc_starts = jnp.cumsum(doc_lengths) - doc_lengths
    doc_ids = doc_of(positions, doc_starts)

    q_cols = w_query.shape[1]
    k_cols = w_key.shape[1]
    w_kv = jnp.concatenate([w_key, w_value], axis=1)
    n_ctx_all = lax.axis_size("ctx")
    ring = [w_kv]
    for shift in range(1, n_ctx_all):
        ring.append(lax.ppermute(w_kv, "ctx", [(i, (i + shift) % n_ctx_all) for i in range(n_ctx_all)]))
    ring = jnp.stack(ring)
    sources = (ctx_index - jnp.arange(n_ctx_all, dtype=jnp.int32)) % n_ctx_all
    w_kv_full = jnp.take(ring, sources, axis=0).reshape(n_ctx_all * tok_rows, w_kv.shape[1])
    kv_local = jnp.dot(tokens, w_kv_full, preferred_element_type=jnp.float32).astype(jnp.bfloat16)
    w_q_full = lax.all_gather(w_query, "ctx", axis=0, tiled=True)
    query_sum = jnp.dot(tokens, w_q_full, preferred_element_type=jnp.float32)

    heads_dev = q_cols // HD
    query = rotate(query_sum.reshape(tok_rows, heads_dev, HD), positions).astype(jnp.bfloat16)

    dd = k_cols // KVH
    group = HEADS // KVH
    kv_local = kv_local.reshape(tok_rows, 2, dd, KVH)
    dest_heads = jnp.arange(n_tp, dtype=jnp.int32) * heads_dev // group
    pieces = jnp.take(kv_local, dest_heads, axis=3)
    pieces = jnp.transpose(pieces, (3, 0, 1, 2))
    got = lax.all_to_all(pieces, "tp", 0, 0, tiled=False)
    kv_own = jnp.transpose(got, (1, 2, 0, 3)).reshape(tok_rows, 2, n_tp * dd)
    key_raw = kv_own[:, 0, :]
    value_own = kv_own[:, 1, :]
    key_rot = rotate(key_raw.astype(jnp.float32)[:, None, :], positions)[:, 0, :].astype(jnp.bfloat16)
    kv_rows_local = jnp.concatenate([key_rot, value_own], axis=1)

    n_ctx = lax.axis_size("ctx")
    back = min(n_ctx - 1, -(-(DOC_MOST - 1) // tok_rows))
    slots = []
    for shift in range(back, 0, -1):
        slots.append(
            lax.ppermute(kv_rows_local, "ctx", [(i, i + shift) for i in range(n_ctx - shift)])
        )
    slots.append(kv_rows_local)
    kv_win = jnp.concatenate(slots, axis=0)
    window = kv_win.shape[0]
    key_start = (ctx_index - back) * tok_rows
    key_win = kv_win[:, :HD]
    value_win = kv_win[:, HD:]
    key_positions = key_start + jnp.arange(window, dtype=jnp.int32)
    key_docs = jnp.where(key_positions >= 0, doc_of(key_positions, doc_starts), -1)

    score_scale = HD ** (-0.5)
    n_split = 2
    part_rows = tok_rows // n_split
    q_parts = jnp.transpose(query, (1, 0, 2)).reshape(heads_dev * n_split, part_rows, HD)
    pos_parts = jnp.tile(positions.reshape(n_split, part_rows), (heads_dev, 1))
    doc_parts = jnp.tile(doc_ids.reshape(n_split, part_rows), (heads_dev, 1))

    def one_part(args):
        q_part, pos_part, doc_part = args
        allowed = (key_positions[None, :] <= pos_part[:, None]) & (key_docs[None, :] == doc_part[:, None])
        scores = jnp.dot(q_part, key_win.T, preferred_element_type=jnp.float32) * score_scale
        masked = jnp.where(allowed, scores, -jnp.inf)
        row_max = jnp.max(masked, axis=-1, keepdims=True)
        expo = jnp.where(allowed, jnp.exp(masked - row_max), 0.0)
        row_total = jnp.sum(expo, axis=-1, keepdims=True)
        mixed = jnp.dot(expo.astype(jnp.bfloat16), value_win, preferred_element_type=jnp.float32)
        return (mixed / row_total).astype(jnp.bfloat16)

    attended = lax.map(one_part, (q_parts, pos_parts, doc_parts))
    attended = attended.reshape(heads_dev, tok_rows, HD)
    attended = jnp.transpose(attended, (1, 0, 2)).reshape(tok_rows, heads_dev * HD)

    w_moved = lax.ppermute(
        w_output,
        ("ctx", "tp"),
        [(c * n_tp + t, t * n_tp + c) for c in range(n_ctx_all) for t in range(n_tp)],
    )
    w_chunk = lax.all_gather(w_moved, "ctx", axis=0, tiled=True)
    from_peers = lax.all_gather(attended, "tp", axis=0, tiled=False)
    w_by_peer = w_chunk.reshape(n_tp, attended.shape[1], w_chunk.shape[1])
    out_chunk = jnp.einsum(
        "trj,tjc->rc", from_peers, w_by_peer, preferred_element_type=jnp.float32
    ).astype(jnp.bfloat16)
    chunk = out_chunk.shape[1]
    out_rows = tok_rows // n_tp
    sent = out_chunk.reshape(n_tp, out_rows, chunk)
    got_rows = lax.all_to_all(sent, "tp", 0, 0, tiled=False)
    return jnp.transpose(got_rows, (1, 0, 2)).reshape(out_rows, n_tp * chunk)


def solution(mesh):
    placed = (P("ctx", None), P(), P("ctx", "tp"), P("ctx", "tp"), P("ctx", "tp"), P("tp", "ctx"))
    return jax.shard_map(
        on_device, mesh=mesh, in_specs=placed, out_specs=P(("ctx", "tp"), None), check_vma=False
    )
```

```python
import jax
import jax.numpy as jnp
from jax import lax
from jax.sharding import PartitionSpec as P

HD = 128
HEADS = 32
KVH = 4
DOC_MOST = 4096

rope_base = 500000.0


def rotate(field, positions):
    half_dim = field.shape[-1] // 2
    inverse_freq = rope_base ** (-2.0 * jnp.arange(half_dim, dtype=jnp.float32) / field.shape[-1])
    angles = positions.astype(jnp.float32)[:, None] * inverse_freq[None, :]
    cosine = jnp.cos(angles)[:, None, :]
    sine_part = jnp.sin(angles)[:, None, :]
    first_half = field[..., :half_dim]
    second_half = field[..., half_dim:]
    return jnp.concatenate(
        [
            first_half * cosine - second_half * sine_part,
            second_half * cosine + first_half * sine_part,
        ],
        axis=-1,
    )


def doc_of(positions, doc_starts):
    return jnp.sum((positions[:, None] >= doc_starts[None, :]).astype(jnp.int32), axis=1)


def on_device(tokens, doc_lengths, w_query, w_key, w_value, w_output):
    tok_rows = tokens.shape[0]
    n_tp = lax.axis_size("tp")
    ctx_index = lax.axis_index("ctx")
    tp_index = lax.axis_index("tp")
    first_row = ctx_index * tok_rows
    positions = first_row + jnp.arange(tok_rows, dtype=jnp.int32)
    doc_starts = jnp.cumsum(doc_lengths) - doc_lengths
    doc_ids = doc_of(positions, doc_starts)

    q_cols = w_query.shape[1]
    k_cols = w_key.shape[1]
    w_kv = jnp.concatenate([w_key, w_value], axis=1)
    n_ctx_all = lax.axis_size("ctx")
    ring = [w_kv]
    for shift in range(1, n_ctx_all):
        ring.append(lax.ppermute(w_kv, "ctx", [(i, (i + shift) % n_ctx_all) for i in range(n_ctx_all)]))
    ring = jnp.stack(ring)
    sources = (ctx_index - jnp.arange(n_ctx_all, dtype=jnp.int32)) % n_ctx_all
    w_kv_full = jnp.take(ring, sources, axis=0).reshape(n_ctx_all * tok_rows, w_kv.shape[1])
    kv_local = jnp.dot(tokens, w_kv_full, preferred_element_type=jnp.float32).astype(jnp.bfloat16)
    w_q_full = lax.all_gather(w_query, "ctx", axis=0, tiled=True)

    heads_dev = q_cols // HD

    dd = k_cols // KVH
    group = HEADS // KVH
    kv_local = kv_local.reshape(tok_rows, 2, dd, KVH)
    dest_heads = jnp.arange(n_tp, dtype=jnp.int32) * heads_dev // group
    pieces = jnp.take(kv_local, dest_heads, axis=3)
    pieces = jnp.transpose(pieces, (3, 0, 1, 2))
    got = lax.all_to_all(pieces, "tp", 0, 0, tiled=False)
    kv_own = jnp.transpose(got, (1, 2, 0, 3)).reshape(tok_rows, 2, n_tp * dd)
    key_raw = kv_own[:, 0, :]
    value_own = kv_own[:, 1, :]
    key_rot = rotate(key_raw.astype(jnp.float32)[:, None, :], positions)[:, 0, :].astype(jnp.bfloat16)
    kv_rows_local = jnp.concatenate([key_rot, value_own], axis=1)

    n_ctx = lax.axis_size("ctx")
    back = min(n_ctx - 1, -(-(DOC_MOST - 1) // tok_rows))
    slots = []
    for shift in range(back, 0, -1):
        slots.append(
            lax.ppermute(kv_rows_local, "ctx", [(i, i + shift) for i in range(n_ctx - shift)])
        )
    slots.append(kv_rows_local)
    slots[0], w_q_full = lax.optimization_barrier((slots[0], w_q_full))
    query_sum = jnp.dot(tokens, w_q_full, preferred_element_type=jnp.float32)
    query = rotate(query_sum.reshape(tok_rows, heads_dev, HD), positions).astype(jnp.bfloat16)
    kv_win = jnp.concatenate(slots, axis=0)
    window = kv_win.shape[0]
    key_start = (ctx_index - back) * tok_rows
    key_win = kv_win[:, :HD]
    value_win = kv_win[:, HD:]
    key_positions = key_start + jnp.arange(window, dtype=jnp.int32)
    key_docs = jnp.where(key_positions >= 0, doc_of(key_positions, doc_starts), -1)

    score_scale = HD ** (-0.5)
    n_split = 2
    part_rows = tok_rows // n_split
    q_parts = jnp.transpose(query, (1, 0, 2)).reshape(heads_dev * n_split, part_rows, HD)
    pos_parts = jnp.tile(positions.reshape(n_split, part_rows), (heads_dev, 1))
    doc_parts = jnp.tile(doc_ids.reshape(n_split, part_rows), (heads_dev, 1))

    def one_part(args):
        q_part, pos_part, doc_part = args
        allowed = (key_positions[None, :] <= pos_part[:, None]) & (key_docs[None, :] == doc_part[:, None])
        scores = jnp.dot(q_part, key_win.T, preferred_element_type=jnp.float32) * score_scale
        masked = jnp.where(allowed, scores, -jnp.inf)
        row_max = jnp.max(masked, axis=-1, keepdims=True)
        expo = jnp.where(allowed, jnp.exp(masked - row_max), 0.0)
        row_total = jnp.sum(expo, axis=-1, keepdims=True)
        mixed = jnp.dot(expo.astype(jnp.bfloat16), value_win, preferred_element_type=jnp.float32)
        return (mixed / row_total).astype(jnp.bfloat16)

    attended = lax.map(one_part, (q_parts, pos_parts, doc_parts))
    attended = attended.reshape(heads_dev, tok_rows, HD)
    attended = jnp.transpose(attended, (1, 0, 2)).reshape(tok_rows, heads_dev * HD)

    w_moved = lax.ppermute(
        w_output,
        ("ctx", "tp"),
        [(c * n_tp + t, t * n_tp + c) for c in range(n_ctx_all) for t in range(n_tp)],
    )
    w_chunk = lax.all_gather(w_moved, "ctx", axis=0, tiled=True)
    attended_all = lax.all_gather(attended, "tp", axis=1, tiled=True)
    out_chunk = jnp.dot(attended_all, w_chunk, preferred_element_type=jnp.float32).astype(jnp.bfloat16)
    chunk = out_chunk.shape[1]
    out_rows = tok_rows // n_tp
    sent = out_chunk.reshape(n_tp, out_rows, chunk)
    got_rows = lax.all_to_all(sent, "tp", 0, 0, tiled=False)
    return jnp.transpose(got_rows, (1, 0, 2)).reshape(out_rows, n_tp * chunk)


def solution(mesh):
    placed = (P("ctx", None), P(), P("ctx", "tp"), P("ctx", "tp"), P("ctx", "tp"), P("tp", "ctx"))
    return jax.shard_map(
        on_device, mesh=mesh, in_specs=placed, out_specs=P(("ctx", "tp"), None), check_vma=False
    )
```

```python
import jax
import jax.numpy as jnp
from jax import lax
from jax.sharding import PartitionSpec as P

HD = 128
HEADS = 32
KVH = 4
DOC_MOST = 4096

rope_base = 500000.0


def rotate(field, positions):
    half_dim = field.shape[-1] // 2
    inverse_freq = rope_base ** (-2.0 * jnp.arange(half_dim, dtype=jnp.float32) / field.shape[-1])
    angles = positions.astype(jnp.float32)[:, None] * inverse_freq[None, :]
    cosine = jnp.cos(angles)[:, None, :]
    sine_part = jnp.sin(angles)[:, None, :]
    first_half = field[..., :half_dim]
    second_half = field[..., half_dim:]
    return jnp.concatenate(
        [
            first_half * cosine - second_half * sine_part,
            second_half * cosine + first_half * sine_part,
        ],
        axis=-1,
    )


def doc_of(positions, doc_starts):
    return jnp.sum((positions[:, None] >= doc_starts[None, :]).astype(jnp.int32), axis=1)


def on_device(tokens, doc_lengths, w_query, w_key, w_value, w_output):
    tok_rows = tokens.shape[0]
    n_tp = lax.axis_size("tp")
    ctx_index = lax.axis_index("ctx")
    tp_index = lax.axis_index("tp")
    first_row = ctx_index * tok_rows
    positions = first_row + jnp.arange(tok_rows, dtype=jnp.int32)
    doc_starts = jnp.cumsum(doc_lengths) - doc_lengths
    doc_ids = doc_of(positions, doc_starts)

    q_cols = w_query.shape[1]
    k_cols = w_key.shape[1]
    w_kv = jnp.concatenate([w_key, w_value], axis=1)
    n_ctx_all = lax.axis_size("ctx")
    ring = [w_kv]
    for shift in range(1, n_ctx_all):
        ring.append(lax.ppermute(w_kv, "ctx", [(i, (i + shift) % n_ctx_all) for i in range(n_ctx_all)]))
    ring = jnp.stack(ring)
    sources = (ctx_index - jnp.arange(n_ctx_all, dtype=jnp.int32)) % n_ctx_all
    w_kv_full = jnp.take(ring, sources, axis=0).reshape(n_ctx_all * tok_rows, w_kv.shape[1])
    kv_local = jnp.dot(tokens, w_kv_full, preferred_element_type=jnp.float32).astype(jnp.bfloat16)
    w_q_full = lax.all_gather(w_query, "ctx", axis=0, tiled=True)
    query_sum = jnp.dot(tokens, w_q_full, preferred_element_type=jnp.float32)

    heads_dev = q_cols // HD
    query = rotate(query_sum.reshape(tok_rows, heads_dev, HD), positions).astype(jnp.bfloat16)

    dd = k_cols // KVH
    group = HEADS // KVH
    kv_local = kv_local.reshape(tok_rows, 2, dd, KVH)
    dest_heads = jnp.arange(n_tp, dtype=jnp.int32) * heads_dev // group
    pieces = jnp.take(kv_local, dest_heads, axis=3)
    pieces = jnp.transpose(pieces, (3, 0, 1, 2))
    got = lax.all_to_all(pieces, "tp", 0, 0, tiled=False)
    kv_own = jnp.transpose(got, (1, 2, 0, 3)).reshape(tok_rows, 2, n_tp * dd)
    key_raw = kv_own[:, 0, :]
    value_own = kv_own[:, 1, :]
    key_rot = rotate(key_raw.astype(jnp.float32)[:, None, :], positions)[:, 0, :].astype(jnp.bfloat16)
    kv_rows_local = jnp.concatenate([key_rot, value_own], axis=1)

    n_ctx = lax.axis_size("ctx")
    back = min(n_ctx - 1, -(-(DOC_MOST - 1) // tok_rows))
    slots = []
    for shift in range(back, 0, -1):
        slots.append(
            lax.ppermute(kv_rows_local, "ctx", [(i, i + shift) for i in range(n_ctx - shift)])
        )
    slots.append(kv_rows_local)
    kv_win = jnp.concatenate(slots, axis=0)
    window = kv_win.shape[0]
    key_start = (ctx_index - back) * tok_rows
    key_win = kv_win[:, :HD]
    value_win = kv_win[:, HD:]
    key_positions = key_start + jnp.arange(window, dtype=jnp.int32)
    key_docs = jnp.where(key_positions >= 0, doc_of(key_positions, doc_starts), -1)

    score_scale = HD ** (-0.5)
    n_split = 1
    part_rows = tok_rows // n_split
    q_parts = jnp.transpose(query, (1, 0, 2)).reshape(heads_dev * n_split, part_rows, HD)
    pos_parts = jnp.tile(positions.reshape(n_split, part_rows), (heads_dev, 1))
    doc_parts = jnp.tile(doc_ids.reshape(n_split, part_rows), (heads_dev, 1))

    def one_part(args):
        q_part, pos_part, doc_part = args
        allowed = (key_positions[None, :] <= pos_part[:, None]) & (key_docs[None, :] == doc_part[:, None])
        scores = jnp.dot(q_part, key_win.T, preferred_element_type=jnp.float32) * score_scale
        masked = jnp.where(allowed, scores, -jnp.inf)
        row_max = jnp.max(masked, axis=-1, keepdims=True)
        expo = jnp.where(allowed, jnp.exp(masked - row_max), 0.0)
        row_total = jnp.sum(expo, axis=-1, keepdims=True)
        mixed = jnp.dot(expo.astype(jnp.bfloat16), value_win, preferred_element_type=jnp.float32)
        return (mixed / row_total).astype(jnp.bfloat16)

    attended = lax.map(one_part, (q_parts, pos_parts, doc_parts))
    attended = attended.reshape(heads_dev, tok_rows, HD)
    attended = jnp.transpose(attended, (1, 0, 2)).reshape(tok_rows, heads_dev * HD)

    w_moved = lax.ppermute(
        w_output,
        ("ctx", "tp"),
        [(c * n_tp + t, t * n_tp + c) for c in range(n_ctx_all) for t in range(n_tp)],
    )
    w_chunk = lax.all_gather(w_moved, "ctx", axis=0, tiled=True)
    attended_all = lax.all_gather(attended, "tp", axis=1, tiled=True)
    out_chunk = jnp.dot(attended_all, w_chunk, preferred_element_type=jnp.float32).astype(jnp.bfloat16)
    chunk = out_chunk.shape[1]
    out_rows = tok_rows // n_tp
    sent = out_chunk.reshape(n_tp, out_rows, chunk)
    got_rows = lax.all_to_all(sent, "tp", 0, 0, tiled=False)
    return jnp.transpose(got_rows, (1, 0, 2)).reshape(out_rows, n_tp * chunk)


def solution(mesh):
    placed = (P("ctx", None), P(), P("ctx", "tp"), P("ctx", "tp"), P("ctx", "tp"), P("tp", "ctx"))
    return jax.shard_map(
        on_device, mesh=mesh, in_specs=placed, out_specs=P(("ctx", "tp"), None), check_vma=False
    )
```

```python
import jax
import jax.numpy as jnp
from jax import lax
from jax.sharding import PartitionSpec as P

HD = 128
HEADS = 32
KVH = 4
DOC_MOST = 4096

rope_base = 500000.0


def rotate(field, positions):
    half_dim = field.shape[-1] // 2
    inverse_freq = rope_base ** (-2.0 * jnp.arange(half_dim, dtype=jnp.float32) / field.shape[-1])
    angles = positions.astype(jnp.float32)[:, None] * inverse_freq[None, :]
    cosine = jnp.cos(angles)[:, None, :]
    sine_part = jnp.sin(angles)[:, None, :]
    first_half = field[..., :half_dim]
    second_half = field[..., half_dim:]
    return jnp.concatenate(
        [
            first_half * cosine - second_half * sine_part,
            second_half * cosine + first_half * sine_part,
        ],
        axis=-1,
    )


def doc_of(positions, doc_starts):
    return jnp.sum((positions[:, None] >= doc_starts[None, :]).astype(jnp.int32), axis=1)


def on_device(tokens, doc_lengths, w_query, w_key, w_value, w_output):
    tok_rows = tokens.shape[0]
    n_tp = lax.axis_size("tp")
    ctx_index = lax.axis_index("ctx")
    tp_index = lax.axis_index("tp")
    first_row = ctx_index * tok_rows
    positions = first_row + jnp.arange(tok_rows, dtype=jnp.int32)
    doc_starts = jnp.cumsum(doc_lengths) - doc_lengths
    doc_ids = doc_of(positions, doc_starts)

    q_cols = w_query.shape[1]
    k_cols = w_key.shape[1]
    w_kv = jnp.concatenate([w_key, w_value], axis=1)
    n_ctx_all = lax.axis_size("ctx")
    ring = [w_kv]
    for shift in range(1, n_ctx_all):
        ring.append(lax.ppermute(w_kv, "ctx", [(i, (i + shift) % n_ctx_all) for i in range(n_ctx_all)]))
    ring = jnp.stack(ring)
    sources = (ctx_index - jnp.arange(n_ctx_all, dtype=jnp.int32)) % n_ctx_all
    w_kv_full = jnp.take(ring, sources, axis=0).reshape(n_ctx_all * tok_rows, w_kv.shape[1])
    kv_local = jnp.dot(tokens, w_kv_full, preferred_element_type=jnp.float32).astype(jnp.bfloat16)
    w_q_full = lax.all_gather(w_query, "ctx", axis=0, tiled=True)
    query_sum = jnp.dot(tokens, w_q_full, preferred_element_type=jnp.float32)

    heads_dev = q_cols // HD
    query = rotate(query_sum.reshape(tok_rows, heads_dev, HD), positions).astype(jnp.bfloat16)

    dd = k_cols // KVH
    group = HEADS // KVH
    kv_local = kv_local.reshape(tok_rows, 2, dd, KVH)
    dest_heads = jnp.arange(n_tp, dtype=jnp.int32) * heads_dev // group
    pieces = jnp.take(kv_local, dest_heads, axis=3)
    pieces = jnp.transpose(pieces, (3, 0, 1, 2))
    got = lax.all_to_all(pieces, "tp", 0, 0, tiled=False)
    kv_own = jnp.transpose(got, (1, 2, 0, 3)).reshape(tok_rows, 2, n_tp * dd)
    key_raw = kv_own[:, 0, :]
    value_own = kv_own[:, 1, :]
    key_rot = rotate(key_raw.astype(jnp.float32)[:, None, :], positions)[:, 0, :].astype(jnp.bfloat16)
    kv_rows_local = jnp.concatenate([key_rot, value_own], axis=1)

    n_ctx = lax.axis_size("ctx")
    back = min(n_ctx - 1, -(-(DOC_MOST - 1) // tok_rows))
    slots = []
    for shift in range(back, 0, -1):
        slots.append(
            lax.ppermute(kv_rows_local, "ctx", [(i, i + shift) for i in range(n_ctx - shift)])
        )
    slots.append(kv_rows_local)
    kv_win = jnp.concatenate(slots, axis=0)
    window = kv_win.shape[0]
    key_start = (ctx_index - back) * tok_rows
    key_win = kv_win[:, :HD]
    value_win = kv_win[:, HD:]
    key_positions = key_start + jnp.arange(window, dtype=jnp.int32)
    key_docs = jnp.where(key_positions >= 0, doc_of(key_positions, doc_starts), -1)

    score_scale = HD ** (-0.5)
    n_split = 4
    part_rows = tok_rows // n_split
    q_parts = jnp.transpose(query, (1, 0, 2)).reshape(heads_dev * n_split, part_rows, HD)
    pos_parts = jnp.tile(positions.reshape(n_split, part_rows), (heads_dev, 1))
    doc_parts = jnp.tile(doc_ids.reshape(n_split, part_rows), (heads_dev, 1))

    def one_part(args):
        q_part, pos_part, doc_part = args
        allowed = (key_positions[None, :] <= pos_part[:, None]) & (key_docs[None, :] == doc_part[:, None])
        scores = jnp.dot(q_part, key_win.T, preferred_element_type=jnp.float32) * score_scale
        masked = jnp.where(allowed, scores, -jnp.inf)
        row_max = jnp.max(masked, axis=-1, keepdims=True)
        expo = jnp.where(allowed, jnp.exp(masked - row_max), 0.0)
        row_total = jnp.sum(expo, axis=-1, keepdims=True)
        mixed = jnp.dot(expo.astype(jnp.bfloat16), value_win, preferred_element_type=jnp.float32)
        return (mixed / row_total).astype(jnp.bfloat16)

    attended = lax.map(one_part, (q_parts, pos_parts, doc_parts))
    attended = attended.reshape(heads_dev, tok_rows, HD)
    attended = jnp.transpose(attended, (1, 0, 2)).reshape(tok_rows, heads_dev * HD)

    w_moved = lax.ppermute(
        w_output,
        ("ctx", "tp"),
        [(c * n_tp + t, t * n_tp + c) for c in range(n_ctx_all) for t in range(n_tp)],
    )
    w_chunk = lax.all_gather(w_moved, "ctx", axis=0, tiled=True)
    attended_all = lax.all_gather(attended, "tp", axis=1, tiled=True)
    out_chunk = jnp.dot(attended_all, w_chunk, preferred_element_type=jnp.float32).astype(jnp.bfloat16)
    chunk = out_chunk.shape[1]
    out_rows = tok_rows // n_tp
    sent = out_chunk.reshape(n_tp, out_rows, chunk)
    got_rows = lax.all_to_all(sent, "tp", 0, 0, tiled=False)
    return jnp.transpose(got_rows, (1, 0, 2)).reshape(out_rows, n_tp * chunk)


def solution(mesh):
    placed = (P("ctx", None), P(), P("ctx", "tp"), P("ctx", "tp"), P("ctx", "tp"), P("tp", "ctx"))
    return jax.shard_map(
        on_device, mesh=mesh, in_specs=placed, out_specs=P(("ctx", "tp"), None), check_vma=False
    )
```

```python
import jax
import jax.numpy as jnp
from jax import lax
from jax.sharding import PartitionSpec as P

HD = 128
HEADS = 32
KVH = 4
DOC_MOST = 4096

rope_base = 500000.0


def rotate(field, positions):
    half_dim = field.shape[-1] // 2
    inverse_freq = rope_base ** (-2.0 * jnp.arange(half_dim, dtype=jnp.float32) / field.shape[-1])
    angles = positions.astype(jnp.float32)[:, None] * inverse_freq[None, :]
    cosine = jnp.cos(angles)[:, None, :]
    sine_part = jnp.sin(angles)[:, None, :]
    first_half = field[..., :half_dim]
    second_half = field[..., half_dim:]
    return jnp.concatenate(
        [
            first_half * cosine - second_half * sine_part,
            second_half * cosine + first_half * sine_part,
        ],
        axis=-1,
    )


def doc_of(positions, doc_starts):
    return jnp.sum((positions[:, None] >= doc_starts[None, :]).astype(jnp.int32), axis=1)


def on_device(tokens, doc_lengths, w_query, w_key, w_value, w_output):
    tok_rows = tokens.shape[0]
    n_tp = lax.axis_size("tp")
    ctx_index = lax.axis_index("ctx")
    tp_index = lax.axis_index("tp")
    first_row = ctx_index * tok_rows
    positions = first_row + jnp.arange(tok_rows, dtype=jnp.int32)
    doc_starts = jnp.cumsum(doc_lengths) - doc_lengths
    doc_ids = doc_of(positions, doc_starts)

    q_cols = w_query.shape[1]
    k_cols = w_key.shape[1]
    w_kv = jnp.concatenate([w_key, w_value], axis=1)
    n_ctx_all = lax.axis_size("ctx")
    ring = [w_kv]
    for shift in range(1, n_ctx_all):
        ring.append(lax.ppermute(w_kv, "ctx", [(i, (i + shift) % n_ctx_all) for i in range(n_ctx_all)]))
    ring = jnp.stack(ring)
    sources = (ctx_index - jnp.arange(n_ctx_all, dtype=jnp.int32)) % n_ctx_all
    w_kv_full = jnp.take(ring, sources, axis=0).reshape(n_ctx_all * tok_rows, w_kv.shape[1])
    kv_local = jnp.dot(tokens, w_kv_full, preferred_element_type=jnp.float32).astype(jnp.bfloat16)
    w_q_full = lax.all_gather(w_query, "ctx", axis=0, tiled=True)
    query_sum = jnp.dot(tokens, w_q_full, preferred_element_type=jnp.float32)

    heads_dev = q_cols // HD
    query = rotate(query_sum.reshape(tok_rows, heads_dev, HD), positions).astype(jnp.bfloat16)

    dd = k_cols // KVH
    group = HEADS // KVH
    kv_local = kv_local.reshape(tok_rows, 2, dd, KVH)
    dest_heads = jnp.arange(n_tp, dtype=jnp.int32) * heads_dev // group
    pieces = jnp.take(kv_local, dest_heads, axis=3)
    pieces = jnp.transpose(pieces, (3, 0, 1, 2))
    got = lax.all_to_all(pieces, "tp", 0, 0, tiled=False)
    kv_own = jnp.transpose(got, (1, 2, 0, 3)).reshape(tok_rows, 2, n_tp * dd)
    key_raw = kv_own[:, 0, :]
    value_own = kv_own[:, 1, :]
    key_rot = rotate(key_raw.astype(jnp.float32)[:, None, :], positions)[:, 0, :].astype(jnp.bfloat16)
    kv_rows_local = jnp.concatenate([key_rot, value_own], axis=1)

    n_ctx = lax.axis_size("ctx")
    back = min(n_ctx - 1, -(-(DOC_MOST - 1) // tok_rows))
    slots = []
    for shift in range(back, 0, -1):
        slots.append(
            lax.ppermute(kv_rows_local, "ctx", [(i, i + shift) for i in range(n_ctx - shift)])
        )
    slots.append(kv_rows_local)
    kv_win = jnp.concatenate(slots, axis=0)
    window = kv_win.shape[0]
    key_start = (ctx_index - back) * tok_rows
    key_win = kv_win[:, :HD]
    value_win = kv_win[:, HD:]
    key_positions = key_start + jnp.arange(window, dtype=jnp.int32)
    key_docs = jnp.where(key_positions >= 0, doc_of(key_positions, doc_starts), -1)

    score_scale = HD ** (-0.5)
    n_split = 2
    part_rows = tok_rows // n_split
    q_parts = jnp.transpose(query, (1, 0, 2)).reshape(heads_dev * n_split, part_rows, HD)
    pos_parts = jnp.tile(positions.reshape(n_split, part_rows), (heads_dev, 1))
    doc_parts = jnp.tile(doc_ids.reshape(n_split, part_rows), (heads_dev, 1))

    def one_part(args):
        q_part, pos_part, doc_part = args
        allowed = (key_positions[None, :] <= pos_part[:, None]) & (key_docs[None, :] == doc_part[:, None])
        scores = jnp.dot(q_part, key_win.T, preferred_element_type=jnp.float32) * score_scale
        masked = jnp.where(allowed, scores, -jnp.inf)
        row_max = jnp.max(masked, axis=-1, keepdims=True)
        expo = jnp.exp(masked - row_max)
        row_total = jnp.sum(expo, axis=-1, keepdims=True)
        mixed = jnp.dot(expo.astype(jnp.bfloat16), value_win, preferred_element_type=jnp.float32)
        return (mixed / row_total).astype(jnp.bfloat16)

    attended = lax.map(one_part, (q_parts, pos_parts, doc_parts))
    attended = attended.reshape(heads_dev, tok_rows, HD)
    attended = jnp.transpose(attended, (1, 0, 2)).reshape(tok_rows, heads_dev * HD)

    w_moved = lax.ppermute(
        w_output,
        ("ctx", "tp"),
        [(c * n_tp + t, t * n_tp + c) for c in range(n_ctx_all) for t in range(n_tp)],
    )
    w_chunk = lax.all_gather(w_moved, "ctx", axis=0, tiled=True)
    attended_all = lax.all_gather(attended, "tp", axis=1, tiled=True)
    out_chunk = jnp.dot(attended_all, w_chunk, preferred_element_type=jnp.float32).astype(jnp.bfloat16)
    chunk = out_chunk.shape[1]
    out_rows = tok_rows // n_tp
    sent = out_chunk.reshape(n_tp, out_rows, chunk)
    got_rows = lax.all_to_all(sent, "tp", 0, 0, tiled=False)
    return jnp.transpose(got_rows, (1, 0, 2)).reshape(out_rows, n_tp * chunk)


def solution(mesh):
    placed = (P("ctx", None), P(), P("ctx", "tp"), P("ctx", "tp"), P("ctx", "tp"), P("tp", "ctx"))
    return jax.shard_map(
        on_device, mesh=mesh, in_specs=placed, out_specs=P(("ctx", "tp"), None), check_vma=False
    )
```

```python
import jax
import jax.numpy as jnp
from jax import lax
from jax.sharding import PartitionSpec as P

HD = 128
HEADS = 32
KVH = 4
DOC_MOST = 4096

rope_base = 500000.0


def rotate(field, positions):
    half_dim = field.shape[-1] // 2
    inverse_freq = rope_base ** (-2.0 * jnp.arange(half_dim, dtype=jnp.float32) / field.shape[-1])
    angles = positions.astype(jnp.float32)[:, None] * inverse_freq[None, :]
    cosine = jnp.cos(angles)[:, None, :]
    sine_part = jnp.sin(angles)[:, None, :]
    first_half = field[..., :half_dim]
    second_half = field[..., half_dim:]
    return jnp.concatenate(
        [
            first_half * cosine - second_half * sine_part,
            second_half * cosine + first_half * sine_part,
        ],
        axis=-1,
    )


def doc_of(positions, doc_starts):
    return jnp.sum((positions[:, None] >= doc_starts[None, :]).astype(jnp.int32), axis=1)


def on_device(tokens, doc_lengths, w_query, w_key, w_value, w_output):
    tok_rows = tokens.shape[0]
    n_tp = lax.axis_size("tp")
    ctx_index = lax.axis_index("ctx")
    tp_index = lax.axis_index("tp")
    first_row = ctx_index * tok_rows
    positions = first_row + jnp.arange(tok_rows, dtype=jnp.int32)
    doc_starts = jnp.cumsum(doc_lengths) - doc_lengths
    doc_ids = doc_of(positions, doc_starts)

    q_cols = w_query.shape[1]
    k_cols = w_key.shape[1]
    w_kv = jnp.concatenate([w_key, w_value], axis=1)
    n_ctx_all = lax.axis_size("ctx")
    ring = [w_kv]
    for shift in range(1, n_ctx_all):
        ring.append(lax.ppermute(w_kv, "ctx", [(i, (i + shift) % n_ctx_all) for i in range(n_ctx_all)]))
    ring = jnp.stack(ring)
    sources = (ctx_index - jnp.arange(n_ctx_all, dtype=jnp.int32)) % n_ctx_all
    w_kv_full = jnp.take(ring, sources, axis=0).reshape(n_ctx_all * tok_rows, w_kv.shape[1])
    kv_local = jnp.dot(tokens, w_kv_full, preferred_element_type=jnp.float32).astype(jnp.bfloat16)
    w_q_full = lax.all_gather(w_query, "ctx", axis=0, tiled=True)
    query_sum = jnp.dot(tokens, w_q_full, preferred_element_type=jnp.float32)

    heads_dev = q_cols // HD
    query = rotate(query_sum.reshape(tok_rows, heads_dev, HD), positions).astype(jnp.bfloat16)

    dd = k_cols // KVH
    group = HEADS // KVH
    kv_local = kv_local.reshape(tok_rows, 2, dd, KVH)
    dest_heads = jnp.arange(n_tp, dtype=jnp.int32) * heads_dev // group
    pieces = jnp.take(kv_local, dest_heads, axis=3)
    pieces = jnp.transpose(pieces, (3, 0, 1, 2))
    got = lax.all_to_all(pieces, "tp", 0, 0, tiled=False)
    kv_own = jnp.transpose(got, (1, 2, 0, 3)).reshape(tok_rows, 2, n_tp * dd)
    key_raw = kv_own[:, 0, :]
    value_own = kv_own[:, 1, :]
    key_rot = rotate(key_raw.astype(jnp.float32)[:, None, :], positions)[:, 0, :].astype(jnp.bfloat16)
    kv_rows_local = jnp.concatenate([key_rot, value_own], axis=1)

    n_ctx = lax.axis_size("ctx")
    back = min(n_ctx - 1, -(-(DOC_MOST - 1) // tok_rows))
    slots = []
    for shift in range(back, 0, -1):
        slots.append(
            lax.ppermute(kv_rows_local, "ctx", [(i, i + shift) for i in range(n_ctx - shift)])
        )
    slots.append(kv_rows_local)
    kv_win = jnp.concatenate(slots, axis=0)
    window = kv_win.shape[0]
    key_start = (ctx_index - back) * tok_rows
    key_win = kv_win[:, :HD]
    value_win = kv_win[:, HD:]
    key_positions = key_start + jnp.arange(window, dtype=jnp.int32)
    key_docs = jnp.where(key_positions >= 0, doc_of(key_positions, doc_starts), -1)

    score_scale = HD ** (-0.5)
    n_split = 4
    part_rows = tok_rows // n_split
    q_parts = jnp.transpose(query, (1, 0, 2)).reshape(heads_dev * n_split, part_rows, HD)
    pos_parts = jnp.tile(positions.reshape(n_split, part_rows), (heads_dev, 1))
    doc_parts = jnp.tile(doc_ids.reshape(n_split, part_rows), (heads_dev, 1))

    def one_part(args):
        q_part, pos_part, doc_part = args
        allowed = (key_positions[None, :] <= pos_part[:, None]) & (key_docs[None, :] == doc_part[:, None])
        scores = jnp.dot(q_part, key_win.T, preferred_element_type=jnp.float32) * score_scale
        masked = jnp.where(allowed, scores, -jnp.inf)
        row_max = jnp.max(masked, axis=-1, keepdims=True)
        expo = jnp.exp(masked - row_max)
        row_total = jnp.sum(expo, axis=-1, keepdims=True)
        mixed = jnp.dot(expo.astype(jnp.bfloat16), value_win, preferred_element_type=jnp.float32)
        return (mixed / row_total).astype(jnp.bfloat16)

    attended = lax.map(one_part, (q_parts, pos_parts, doc_parts))
    attended = attended.reshape(heads_dev, tok_rows, HD)
    attended = jnp.transpose(attended, (1, 0, 2)).reshape(tok_rows, heads_dev * HD)

    w_moved = lax.ppermute(
        w_output,
        ("ctx", "tp"),
        [(c * n_tp + t, t * n_tp + c) for c in range(n_ctx_all) for t in range(n_tp)],
    )
    w_chunk = lax.all_gather(w_moved, "ctx", axis=0, tiled=True)
    attended_all = lax.all_gather(attended, "tp", axis=1, tiled=True)
    out_chunk = jnp.dot(attended_all, w_chunk, preferred_element_type=jnp.float32).astype(jnp.bfloat16)
    chunk = out_chunk.shape[1]
    out_rows = tok_rows // n_tp
    sent = out_chunk.reshape(n_tp, out_rows, chunk)
    got_rows = lax.all_to_all(sent, "tp", 0, 0, tiled=False)
    return jnp.transpose(got_rows, (1, 0, 2)).reshape(out_rows, n_tp * chunk)


def solution(mesh):
    placed = (P("ctx", None), P(), P("ctx", "tp"), P("ctx", "tp"), P("ctx", "tp"), P("tp", "ctx"))
    return jax.shard_map(
        on_device, mesh=mesh, in_specs=placed, out_specs=P(("ctx", "tp"), None), check_vma=False
    )
```

```python
import jax
import jax.numpy as jnp
from jax import lax
from jax.sharding import PartitionSpec as P

HD = 128
HEADS = 32
KVH = 4
DOC_MOST = 4096

rope_base = 500000.0


def rotate(field, positions):
    half_dim = field.shape[-1] // 2
    inverse_freq = rope_base ** (-2.0 * jnp.arange(half_dim, dtype=jnp.float32) / field.shape[-1])
    angles = positions.astype(jnp.float32)[:, None] * inverse_freq[None, :]
    cosine = jnp.cos(angles)[:, None, :]
    sine_part = jnp.sin(angles)[:, None, :]
    first_half = field[..., :half_dim]
    second_half = field[..., half_dim:]
    return jnp.concatenate(
        [
            first_half * cosine - second_half * sine_part,
            second_half * cosine + first_half * sine_part,
        ],
        axis=-1,
    )


def doc_of(positions, doc_starts):
    return jnp.sum((positions[:, None] >= doc_starts[None, :]).astype(jnp.int32), axis=1)


def on_device(tokens, doc_lengths, w_query, w_key, w_value, w_output):
    tok_rows = tokens.shape[0]
    n_tp = lax.axis_size("tp")
    ctx_index = lax.axis_index("ctx")
    tp_index = lax.axis_index("tp")
    first_row = ctx_index * tok_rows
    positions = first_row + jnp.arange(tok_rows, dtype=jnp.int32)
    doc_starts = jnp.cumsum(doc_lengths) - doc_lengths
    doc_ids = doc_of(positions, doc_starts)

    q_cols = w_query.shape[1]
    k_cols = w_key.shape[1]
    w_kv = jnp.concatenate([w_key, w_value], axis=1)
    n_ctx_all = lax.axis_size("ctx")
    ring = [w_kv]
    for shift in range(1, n_ctx_all):
        ring.append(lax.ppermute(w_kv, "ctx", [(i, (i + shift) % n_ctx_all) for i in range(n_ctx_all)]))
    ring = jnp.stack(ring)
    sources = (ctx_index - jnp.arange(n_ctx_all, dtype=jnp.int32)) % n_ctx_all
    w_kv_full = jnp.take(ring, sources, axis=0).reshape(n_ctx_all * tok_rows, w_kv.shape[1])
    kv_local = jnp.dot(tokens, w_kv_full, preferred_element_type=jnp.float32).astype(jnp.bfloat16)
    w_q_full = lax.all_gather(w_query, "ctx", axis=0, tiled=True)
    query_sum = jnp.dot(tokens, w_q_full, preferred_element_type=jnp.float32)

    heads_dev = q_cols // HD
    query = rotate(query_sum.reshape(tok_rows, heads_dev, HD), positions).astype(jnp.bfloat16)

    dd = k_cols // KVH
    group = HEADS // KVH
    kv_local = kv_local.reshape(tok_rows, 2, dd, KVH)
    dest_heads = jnp.arange(n_tp, dtype=jnp.int32) * heads_dev // group
    pieces = jnp.take(kv_local, dest_heads, axis=3)
    pieces = jnp.transpose(pieces, (3, 0, 1, 2))
    got = lax.all_to_all(pieces, "tp", 0, 0, tiled=False)
    kv_own = jnp.transpose(got, (1, 2, 0, 3)).reshape(tok_rows, 2, n_tp * dd)
    key_raw = kv_own[:, 0, :]
    value_own = kv_own[:, 1, :]
    key_rot = rotate(key_raw.astype(jnp.float32)[:, None, :], positions)[:, 0, :].astype(jnp.bfloat16)
    kv_rows_local = jnp.concatenate([key_rot, value_own], axis=1)

    n_ctx = lax.axis_size("ctx")
    back = min(n_ctx - 1, -(-(DOC_MOST - 1) // tok_rows))
    slots = []
    for shift in range(back, 0, -1):
        slots.append(
            lax.ppermute(kv_rows_local, "ctx", [(i, i + shift) for i in range(n_ctx - shift)])
        )
    slots.append(kv_rows_local)
    kv_win = jnp.concatenate(slots, axis=0)
    window = kv_win.shape[0]
    key_start = (ctx_index - back) * tok_rows
    key_win = kv_win[:, :HD]
    value_win = kv_win[:, HD:]
    key_positions = key_start + jnp.arange(window, dtype=jnp.int32)
    key_docs = jnp.where(key_positions >= 0, doc_of(key_positions, doc_starts), -1)

    score_scale = HD ** (-0.5)
    n_split = 1
    part_rows = tok_rows // n_split
    q_parts = jnp.transpose(query, (1, 0, 2)).reshape(heads_dev * n_split, part_rows, HD)
    pos_parts = jnp.tile(positions.reshape(n_split, part_rows), (heads_dev, 1))
    doc_parts = jnp.tile(doc_ids.reshape(n_split, part_rows), (heads_dev, 1))

    def one_part(args):
        q_part, pos_part, doc_part = args
        allowed = (key_positions[None, :] <= pos_part[:, None]) & (key_docs[None, :] == doc_part[:, None])
        scores = jnp.dot(q_part, key_win.T, preferred_element_type=jnp.float32) * score_scale
        masked = jnp.where(allowed, scores, -jnp.inf)
        row_max = jnp.max(masked, axis=-1, keepdims=True)
        expo = jnp.exp(masked - row_max)
        row_total = jnp.sum(expo, axis=-1, keepdims=True)
        mixed = jnp.dot(expo.astype(jnp.bfloat16), value_win, preferred_element_type=jnp.float32)
        return (mixed / row_total).astype(jnp.bfloat16)

    attended = lax.map(one_part, (q_parts, pos_parts, doc_parts))
    attended = attended.reshape(heads_dev, tok_rows, HD)
    attended = jnp.transpose(attended, (1, 0, 2)).reshape(tok_rows, heads_dev * HD)

    w_moved = lax.ppermute(
        w_output,
        ("ctx", "tp"),
        [(c * n_tp + t, t * n_tp + c) for c in range(n_ctx_all) for t in range(n_tp)],
    )
    w_chunk = lax.all_gather(w_moved, "ctx", axis=0, tiled=True)
    attended_all = lax.all_gather(attended, "tp", axis=1, tiled=True)
    out_chunk = jnp.dot(attended_all, w_chunk, preferred_element_type=jnp.float32).astype(jnp.bfloat16)
    chunk = out_chunk.shape[1]
    out_rows = tok_rows // n_tp
    sent = out_chunk.reshape(n_tp, out_rows, chunk)
    got_rows = lax.all_to_all(sent, "tp", 0, 0, tiled=False)
    return jnp.transpose(got_rows, (1, 0, 2)).reshape(out_rows, n_tp * chunk)


def solution(mesh):
    placed = (P("ctx", None), P(), P("ctx", "tp"), P("ctx", "tp"), P("ctx", "tp"), P("tp", "ctx"))
    return jax.shard_map(
        on_device, mesh=mesh, in_specs=placed, out_specs=P(("ctx", "tp"), None), check_vma=False
    )
```
